256 devices in a mesh: tm: 16 (over z, core), row: 2 (over x_hi), col: 8 (over y, x_lo).
Axes of the slice: x: 4 (x_hi: 2, x_lo: 2; x = x_hi * 2 + x_lo), y: 4, z: 8, core: 2. Of those that a mesh axis runs over, the one named last changes fastest.
Arguments:
- latents: bfloat16 [32, 64, 40960], P('tm', 'row', 'col'), may hold values from -6 to 6
- w_qkv: bfloat16 [320, 960], replicated, may hold values from -4 to 4
- w_out: bfloat16 [320, 320], replicated, may hold values from -0.3125 to 0.3125
- conv_weight: float32 [9, 320], replicated, may hold values from -1.8 to 1.8
Outputs:
- result: bfloat16 [32, 64, 40960], P('tm', 'row', 'col')
The draws below stay inside these ranges and needn't reach their ends.
All inputs are finite; a program needn't handle non-finite values.
Results may differ from the reference program's by a relative error of at most 0.013.
Values may be sent and summed in bfloat16 or wider, within the bound.
No kernel may reach another device: no remote copies, remote signals or barrier semaphores. Data moves between devices by JAX's collectives and lax.ppermute only.
A program may use at most 64 MiB of HBM per device.

```python
import jax
import jax.numpy as jnp
from jax import lax

C = 320
HEAD_DIM = 64
FRAMES = 32
HEIGHT = 64
WIDTH = 128


def draw_w_qkv(key, part):
    base = jax.random.normal(key, (C, 3 * C), jnp.float32) * C ** (-0.5)
    return jnp.clip(base, -4.0, 4.0).astype(jnp.bfloat16)


def levels(own_key, shape, cuts, smallest, largest):
    gain, own = 1.0, jax.random.fold_in(own_key, 6)
    for axis_at, shards_of in cuts:
        steps = jnp.exp(jax.random.uniform(jax.random.fold_in(own, axis_at), (shards_of,), jnp.float32, smallest / len(cuts), largest / len(cuts)))
        gain = gain * jnp.repeat(steps, shape[axis_at] // shards_of).reshape([-1 if axis == axis_at else 1 for axis in range(len(shape))])
    return gain


def centred(stream_key, dims, deviation, bound, split=(), kind=jnp.bfloat16):
    drawn = jax.random.normal(stream_key, dims, jnp.float32) * deviation
    if len(split) > 0:
        drawn = levels(stream_key, dims, split, -0.22, 0.18) * drawn
    return jnp.clip(drawn, min=-bound, max=bound).astype(kind)


def setup_inputs(seed: int = 0) -> dict:
    streams_of = jax.random.split(jax.random.key(seed), 5)
    latents = centred(streams_of[0], (FRAMES, HEIGHT, WIDTH * C), 1.0, 6.0, ((0, 16), (1, 2), (2, 8)))
    w_qkv = draw_w_qkv(jax.random.fold_in(streams_of[4], 71), 0)
    w_out = centred(streams_of[2], (C, C), C ** -0.5, 0.3125)
    conv_weight = centred(streams_of[3], (9, C), 0.3, 1.8, (), jnp.float32)
    return dict(latents=latents, w_qkv=w_qkv, w_out=w_out, conv_weight=conv_weight)


def layer_norm(flat):
    mean = lax.optimization_barrier(jnp.mean(flat, axis=-1, keepdims=True))
    cent = flat - mean
    var = lax.optimization_barrier(jnp.mean(cent * cent, axis=-1, keepdims=True))
    return (cent * lax.rsqrt(var + 1e-05)).astype(jnp.bfloat16)

def window_attend(query, wide, first, total, heads, head_dim):
    frames = query.shape[0]
    points = query.shape[1]
    chans = heads * head_dim
    q_four = query.reshape(frames, points, heads, head_dim)
    scores = []
    values = []
    for shift_d in range(5):
        keys = wide[shift_d:shift_d + frames, :, :chans].reshape(frames, points, heads, head_dim)
        vals = wide[shift_d:shift_d + frames, :, chans:].reshape(frames, points, heads, head_dim)
        score = jnp.einsum('fphd,fphd->fph', q_four, keys, preferred_element_type=jnp.float32) * head_dim ** (-0.5)
        where_t = first + jnp.arange(frames, dtype=jnp.int32) + (shift_d - 2)
        valid = (where_t >= 0) & (where_t < total)
        scores.append(jnp.where(valid[:, None, None], score, jnp.float32(-1e+30)))
        values.append(vals)
    stacked = jnp.stack(scores, 0)
    top = lax.optimization_barrier(jnp.max(stacked, axis=0, keepdims=True))
    expo = jnp.exp(stacked - top)
    weights = (expo / lax.optimization_barrier(jnp.sum(expo, axis=0, keepdims=True))).astype(jnp.bfloat16)
    mixed = jnp.zeros((frames, points, heads, head_dim), jnp.float32)
    for shift_d in range(5):
        mixed = mixed + weights[shift_d].astype(jnp.float32)[..., None] * values[shift_d].astype(jnp.float32)
    return mixed.astype(jnp.bfloat16).reshape(frames * points, chans)

def reference(latents, w_qkv, w_out, conv_weight):
    frames, height, merged = latents.shape
    chans = w_out.shape[0]
    cols = merged // chans
    heads = chans // HEAD_DIM
    x_four = jnp.moveaxis(latents.reshape(frames, height, cols, chans), 1, 0)

    def strip(cells):
        flat = cells.reshape(frames * cols, chans).astype(jnp.float32)
        normed = layer_norm(flat)
        qkv = jnp.dot(normed, w_qkv, preferred_element_type=jnp.float32).astype(jnp.bfloat16)
        qkv = qkv.reshape(frames, cols, 3 * chans)
        pairs = qkv[:, :, chans:]
        zeros = jnp.zeros((2, cols, 2 * chans), jnp.bfloat16)
        wide = jnp.concatenate([zeros, pairs, zeros], 0)
        attended = window_attend(qkv[:, :, :chans], wide, jnp.int32(0), frames, heads, HEAD_DIM)
        proj = jnp.dot(attended, w_out, preferred_element_type=jnp.float32)
        return (flat + proj).astype(jnp.bfloat16).reshape(frames, cols, chans)
    hidden = jnp.moveaxis(lax.map(strip, x_four), 0, 1)

    def conv_frame(frame):
        padded = jnp.pad(frame, ((1, 1), (1, 1), (0, 0)))
        acc = frame.astype(jnp.float32)
        for tap_a in range(3):
            for tap_b in range(3):
                acc = acc + padded[tap_a:tap_a + height, tap_b:tap_b + cols, :].astype(jnp.float32) * conv_weight[3 * tap_a + tap_b]
        return acc.astype(jnp.bfloat16)
    result = lax.map(conv_frame, hidden)
    return result.reshape(frames, height, cols * chans)
```

```python
import functools

import jax
import jax.numpy as jnp
from jax import lax
from jax.experimental import pallas as pl
from jax.experimental.pallas import tpu as pltpu
from jax.sharding import PartitionSpec as P

HEAD_DIM = 64
BLOCK = 128


def layer_norm(flat):
    mean = jnp.mean(flat, axis=-1, keepdims=True)
    cent = flat - mean
    var = jnp.mean(cent * cent, axis=-1, keepdims=True)
    return (cent * lax.rsqrt(var + 1e-05)).astype(jnp.bfloat16)


def attend_kernel(valid_ref, prev_ref, own_ref, next_ref, wqkv_ref, wout_ref, hsum_ref, out_ref):
    chans = wout_ref.shape[0]
    block = own_ref.shape[1]
    frames = [prev_ref[0], prev_ref[1], own_ref[0], own_ref[1], next_ref[0], next_ref[1]]
    normed = [layer_norm(f.astype(jnp.float32)) for f in frames]
    own_n = jnp.concatenate([normed[2], normed[3]], axis=0)
    qkv = jnp.dot(own_n, wqkv_ref[...], preferred_element_type=jnp.float32).astype(jnp.bfloat16)
    nb_n = jnp.concatenate([normed[0], normed[1], normed[4], normed[5]], axis=0)
    kv_nb = jnp.dot(
        nb_n, wqkv_ref[:, chans:], preferred_element_type=jnp.float32
    ).astype(jnp.bfloat16)
    keys = [None] * 6
    vals = [None] * 6
    for w, slot in ((0, 0), (1, 1), (4, 2), (5, 3)):
        keys[w] = kv_nb[slot * block : (slot + 1) * block, :chans]
        vals[w] = kv_nb[slot * block : (slot + 1) * block, chans:]
    for t in range(2):
        keys[2 + t] = qkv[t * block : (t + 1) * block, chans : 2 * chans]
        vals[2 + t] = qkv[t * block : (t + 1) * block, 2 * chans :]
    hsum = hsum_ref[...]
    outs = []
    for t in range(2):
        q = qkv[t * block : (t + 1) * block, :chans].astype(jnp.float32)
        scores = []
        for d in range(5):
            w = t + d
            prod = q * keys[w].astype(jnp.float32)
            hi = prod.astype(jnp.bfloat16)
            lo = (prod - hi.astype(jnp.float32)).astype(jnp.bfloat16)
            score = jnp.dot(hi, hsum, preferred_element_type=jnp.float32) + jnp.dot(
                lo, hsum, preferred_element_type=jnp.float32
            )
            score = score * (HEAD_DIM ** (-0.5))
            score = jnp.where(valid_ref[w] > 0, score, jnp.float32(-1e30))
            scores.append(score)
        top = scores[0]
        for s in scores[1:]:
            top = jnp.maximum(top, s)
        expo = [jnp.exp(s - top) for s in scores]
        denom = expo[0]
        for e in expo[1:]:
            denom = denom + e
        mixed = None
        for d in range(5):
            weight = (expo[d] / denom).astype(jnp.bfloat16).astype(jnp.float32)
            term = weight * vals[t + d].astype(jnp.float32)
            mixed = term if mixed is None else mixed + term
        outs.append(mixed.astype(jnp.bfloat16))
    attended = jnp.concatenate(outs, axis=0)
    proj = jnp.dot(attended, wout_ref[...], preferred_element_type=jnp.float32)
    xown = jnp.concatenate([own_ref[0], own_ref[1]], axis=0).astype(jnp.float32)
    hidden = (xown + proj).astype(jnp.bfloat16)
    out_ref[0] = hidden[:block]
    out_ref[1] = hidden[block:]


def attend(valid, prev, own, nxt, w_qkv, w_out, hsum):
    frames, points, chans = own.shape
    grid = (points // BLOCK,)
    cell_spec = pl.BlockSpec((frames, BLOCK, chans), lambda i: (0, i, 0))
    full = lambda shape: pl.BlockSpec(shape, lambda i: (0, 0))
    return pl.pallas_call(
        attend_kernel,
        grid=grid,
        in_specs=[
            pl.BlockSpec(memory_space=pltpu.SMEM),
            cell_spec,
            cell_spec,
            cell_spec,
            full(w_qkv.shape),
            full(w_out.shape),
            full(hsum.shape),
        ],
        out_specs=cell_spec,
        out_shape=jax.ShapeDtypeStruct(own.shape, jnp.bfloat16),
    )(valid, prev, own, nxt, w_qkv, w_out, hsum)


def shift(x, axis, step):
    count = lax.axis_size(axis)
    if step > 0:
        pairs = [(i, i + 1) for i in range(count - 1)]
    else:
        pairs = [(i + 1, i) for i in range(count - 1)]
    return lax.ppermute(x, axis, pairs)


def shift2(x, rstep, cstep):
    rows = lax.axis_size("row")
    cols = lax.axis_size("col")
    pairs = []
    for r in range(rows):
        for c in range(cols):
            rr, cc = r + rstep, c + cstep
            if 0 <= rr < rows and 0 <= cc < cols:
                pairs.append((r * cols + c, rr * cols + cc))
    return lax.ppermute(x, ("row", "col"), pairs)


def body(latents, w_qkv, w_out, conv_weight):
    frames, rows, merged = latents.shape
    chans = w_out.shape[0]
    cols = merged // chans
    points = rows * cols
    x_prev = shift(latents, "tm", 1)
    x_next = shift(latents, "tm", -1)
    first = lax.axis_index("tm") * frames
    total = lax.axis_size("tm") * frames
    where_t = first + jnp.arange(6, dtype=jnp.int32) - 2
    valid = ((where_t >= 0) & (where_t < total)).astype(jnp.int32)
    group = jnp.arange(chans, dtype=jnp.int32) // HEAD_DIM
    hsum = (group[:, None] == group[None, :]).astype(jnp.bfloat16)
    cells = lambda a: a.reshape(frames, points, chans)
    hidden = attend(valid, cells(x_prev), cells(latents), cells(x_next), w_qkv, w_out, hsum)
    hid = hidden.reshape(frames, rows, merged)

    top_row = hid[:, :1, :]
    bot_row = hid[:, rows - 1 :, :]
    left_col = hid[:, :, :chans]
    right_col = hid[:, :, merged - chans :]
    halo_top = shift(bot_row, "row", 1)
    halo_bot = shift(top_row, "row", -1)
    halo_left = shift(right_col, "col", 1)
    halo_right = shift(left_col, "col", -1)
    c_tl = shift2(hid[:, rows - 1 :, merged - chans :], 1, 1)
    c_tr = shift2(hid[:, rows - 1 :, :chans], 1, -1)
    c_bl = shift2(hid[:, :1, merged - chans :], -1, 1)
    c_br = shift2(hid[:, :1, :chans], -1, -1)
    padded = jnp.concatenate(
        [
            jnp.concatenate([c_tl, halo_top, c_tr], axis=2),
            jnp.concatenate([halo_left, hid, halo_right], axis=2),
            jnp.concatenate([c_bl, halo_bot, c_br], axis=2),
        ],
        axis=1,
    )
    taps = jnp.tile(conv_weight, (1, cols))
    acc = hid.astype(jnp.float32)
    for tap_a in range(3):
        for tap_b in range(3):
            acc = (
                acc
                + padded[:, tap_a : tap_a + rows, tap_b * chans : tap_b * chans + merged].astype(
                    jnp.float32
                )
                * taps[3 * tap_a + tap_b]
            )
    return acc.astype(jnp.bfloat16)


def solution(mesh):
    placed = (P("tm", "row", "col"), P(), P(), P())
    return jax.shard_map(
        body, mesh=mesh, in_specs=placed, out_specs=P("tm", "row", "col"), check_vma=False
    )
```

```python
import functools

import jax
import jax.numpy as jnp
from jax import lax
from jax.experimental import pallas as pl
from jax.experimental.pallas import tpu as pltpu
from jax.sharding import PartitionSpec as P

HEAD_DIM = 64
BLOCK = 128


def layer_norm(flat):
    mean = jnp.mean(flat, axis=-1, keepdims=True)
    cent = flat - mean
    var = jnp.mean(cent * cent, axis=-1, keepdims=True)
    return (cent * lax.rsqrt(var + 1e-05)).astype(jnp.bfloat16)


def attend_kernel(valid_ref, prev_ref, own_ref, next_ref, wqkv_ref, wout_ref, out_ref):
    chans = wout_ref.shape[0]
    heads = chans // HEAD_DIM
    block = own_ref.shape[1]
    frames = [prev_ref[0], prev_ref[1], own_ref[0], own_ref[1], next_ref[0], next_ref[1]]
    normed = [layer_norm(f.astype(jnp.float32)) for f in frames]
    nt = (((1,), (1,)), ((), ()))
    own_n = jnp.concatenate([normed[2], normed[3]], axis=0)
    qkv = lax.dot_general(
        wqkv_ref[...], own_n, nt, preferred_element_type=jnp.float32
    ).astype(jnp.bfloat16)
    nb_n = jnp.concatenate([normed[0], normed[1], normed[4], normed[5]], axis=0)
    kv_nb = lax.dot_general(
        wqkv_ref[chans:, :], nb_n, nt, preferred_element_type=jnp.float32
    ).astype(jnp.bfloat16)
    keys = [None] * 6
    vals = [None] * 6
    for w, slot in ((0, 0), (1, 1), (4, 2), (5, 3)):
        keys[w] = kv_nb[:chans, slot * block : (slot + 1) * block]
        vals[w] = kv_nb[chans:, slot * block : (slot + 1) * block]
    for t in range(2):
        keys[2 + t] = qkv[chans : 2 * chans, t * block : (t + 1) * block]
        vals[2 + t] = qkv[2 * chans :, t * block : (t + 1) * block]
    outs = []
    for t in range(2):
        q = qkv[:chans, t * block : (t + 1) * block].astype(jnp.float32)
        scores = []
        for d in range(5):
            w = t + d
            prod = q * keys[w].astype(jnp.float32)
            score = jnp.sum(prod.reshape(heads, HEAD_DIM, block), axis=1)
            score = score * (HEAD_DIM ** (-0.5))
            score = jnp.where(valid_ref[w] > 0, score, jnp.float32(-1e30))
            scores.append(score)
        top = scores[0]
        for s in scores[1:]:
            top = jnp.maximum(top, s)
        expo = [jnp.exp(s - top) for s in scores]
        denom = expo[0]
        for e in expo[1:]:
            denom = denom + e
        mixed = None
        for d in range(5):
            weight = (expo[d] / denom).astype(jnp.bfloat16).astype(jnp.float32)
            wide = jnp.broadcast_to(weight[:, None, :], (heads, HEAD_DIM, block)).reshape(chans, block)
            term = wide * vals[t + d].astype(jnp.float32)
            mixed = term if mixed is None else mixed + term
        outs.append(mixed.astype(jnp.bfloat16))
    attended = jnp.concatenate(outs, axis=1)
    tn = (((0,), (0,)), ((), ()))
    proj = lax.dot_general(attended, wout_ref[...], tn, preferred_element_type=jnp.float32)
    xown = jnp.concatenate([own_ref[0], own_ref[1]], axis=0).astype(jnp.float32)
    hidden = (xown + proj).astype(jnp.bfloat16)
    out_ref[0] = hidden[:block]
    out_ref[1] = hidden[block:]


def attend(valid, prev, own, nxt, w_qkv, w_out):
    frames, points, chans = own.shape
    w_qkv = w_qkv.T
    grid = (points // BLOCK,)
    cell_spec = pl.BlockSpec((frames, BLOCK, chans), lambda i: (0, i, 0))
    full = lambda shape: pl.BlockSpec(shape, lambda i: (0, 0))
    return pl.pallas_call(
        attend_kernel,
        grid=grid,
        in_specs=[
            pl.BlockSpec(memory_space=pltpu.SMEM),
            cell_spec,
            cell_spec,
            cell_spec,
            full(w_qkv.shape),
            full(w_out.shape),
        ],
        out_specs=cell_spec,
        out_shape=jax.ShapeDtypeStruct(own.shape, jnp.bfloat16),
    )(valid, prev, own, nxt, w_qkv, w_out)


def shift(x, axis, step):
    count = lax.axis_size(axis)
    if step > 0:
        pairs = [(i, i + 1) for i in range(count - 1)]
    else:
        pairs = [(i + 1, i) for i in range(count - 1)]
    return lax.ppermute(x, axis, pairs)


def body(latents, w_qkv, w_out, conv_weight):
    frames, rows, merged = latents.shape
    chans = w_out.shape[0]
    cols = merged // chans
    points = rows * cols
    x_prev = shift(latents, "tm", 1)
    x_next = shift(latents, "tm", -1)
    first = lax.axis_index("tm") * frames
    total = lax.axis_size("tm") * frames
    where_t = first + jnp.arange(6, dtype=jnp.int32) - 2
    valid = ((where_t >= 0) & (where_t < total)).astype(jnp.int32)
    cells = lambda a: a.reshape(frames, points, chans)
    hidden = attend(valid, cells(x_prev), cells(latents), cells(x_next), w_qkv, w_out)
    hid = hidden.reshape(frames, rows, merged)

    halo_top = shift(hid[:, rows - 1 :, :], "row", 1)
    halo_bot = shift(hid[:, :1, :], "row", -1)
    tall = jnp.concatenate([halo_top, hid, halo_bot], axis=1)
    halo_left = shift(tall[:, :, merged - chans :], "col", 1)
    halo_right = shift(tall[:, :, :chans], "col", -1)
    padded = jnp.concatenate([halo_left, tall, halo_right], axis=2)
    taps = jnp.tile(conv_weight, (1, cols))
    acc = hid.astype(jnp.float32)
    for tap_a in range(3):
        for tap_b in range(3):
            acc = (
                acc
                + padded[:, tap_a : tap_a + rows, tap_b * chans : tap_b * chans + merged].astype(
                    jnp.float32
                )
                * taps[3 * tap_a + tap_b]
            )
    return acc.astype(jnp.bfloat16)


def solution(mesh):
    placed = (P("tm", "row", "col"), P(), P(), P())
    return jax.shard_map(
        body, mesh=mesh, in_specs=placed, out_specs=P("tm", "row", "col"), check_vma=False
    )
```

```python
import jax
import jax.numpy as jnp
from jax import lax
from jax.experimental import pallas as pl
from jax.experimental.pallas import tpu as pltpu
from jax.sharding import PartitionSpec as P


HEAD_DIM = 64
BLOCK = 128


def layer_norm(flat):
    mean = jnp.mean(flat, axis=-1, keepdims=True)
    cent = flat - mean
    var = jnp.mean(cent * cent, axis=-1, keepdims=True)
    return (cent * lax.rsqrt(var + 1e-05)).astype(jnp.bfloat16)


def attend_kernel(valid_ref, prev_ref, own_ref, next_ref, wqkv_ref, wout_ref, out_ref):
    chans = wout_ref.shape[0]
    heads = chans // HEAD_DIM
    block = own_ref.shape[1]
    frames = [prev_ref[0], prev_ref[1], own_ref[0], own_ref[1], next_ref[0], next_ref[1]]
    normed = [layer_norm(f.astype(jnp.float32)) for f in frames]
    nt = (((1,), (1,)), ((), ()))
    own_n = jnp.concatenate([normed[2], normed[3]], axis=0)
    qkv = lax.dot_general(
        wqkv_ref[...], own_n, nt, preferred_element_type=jnp.float32
    ).astype(jnp.bfloat16)
    nb_n = jnp.concatenate([normed[0], normed[1], normed[4], normed[5]], axis=0)
    kv_nb = lax.dot_general(
        wqkv_ref[chans:, :], nb_n, nt, preferred_element_type=jnp.float32
    ).astype(jnp.bfloat16)
    keys = [None] * 6
    vals = [None] * 6
    for w, slot in ((0, 0), (1, 1), (4, 2), (5, 3)):
        keys[w] = kv_nb[:chans, slot * block : (slot + 1) * block]
        vals[w] = kv_nb[chans:, slot * block : (slot + 1) * block]
    for t in range(2):
        keys[2 + t] = qkv[chans : 2 * chans, t * block : (t + 1) * block]
        vals[2 + t] = qkv[2 * chans :, t * block : (t + 1) * block]
    outs = []
    for t in range(2):
        q = qkv[:chans, t * block : (t + 1) * block].astype(jnp.float32)
        scores = []
        for d in range(5):
            w = t + d
            prod = q * keys[w].astype(jnp.float32)
            score = jnp.sum(prod.reshape(heads, HEAD_DIM, block), axis=1)
            score = score * (HEAD_DIM ** (-0.5))
            score = jnp.where(valid_ref[w] > 0, score, jnp.float32(-1e30))
            scores.append(score)
        top = scores[0]
        for s in scores[1:]:
            top = jnp.maximum(top, s)
        expo = [jnp.exp(s - top) for s in scores]
        denom = expo[0]
        for e in expo[1:]:
            denom = denom + e
        mixed = None
        for d in range(5):
            weight = (expo[d] / denom).astype(jnp.bfloat16).astype(jnp.float32)
            wide = jnp.broadcast_to(weight[:, None, :], (heads, HEAD_DIM, block)).reshape(chans, block)
            term = wide * vals[t + d].astype(jnp.float32)
            mixed = term if mixed is None else mixed + term
        outs.append(mixed.astype(jnp.bfloat16))
    attended = jnp.concatenate(outs, axis=1)
    tn = (((0,), (0,)), ((), ()))
    proj = lax.dot_general(attended, wout_ref[...], tn, preferred_element_type=jnp.float32)
    xown = jnp.concatenate([own_ref[0], own_ref[1]], axis=0).astype(jnp.float32)
    hidden = (xown + proj).astype(jnp.bfloat16)
    out_ref[0] = hidden[:block]
    out_ref[1] = hidden[block:]


def attend(valid, prev, own, nxt, w_qkv, w_out, start=0, count=None):
    frames, points, chans = own.shape
    count = points if count is None else count
    w_qkv = w_qkv.T
    grid = (count // BLOCK,)
    assert count % BLOCK == 0 and start % BLOCK == 0
    base = start // BLOCK
    cell_spec = pl.BlockSpec((frames, BLOCK, chans), lambda i: (0, i + base, 0))
    out_spec = pl.BlockSpec((frames, BLOCK, chans), lambda i: (0, i, 0))
    full = lambda shape: pl.BlockSpec(shape, lambda i: (0, 0))
    return pl.pallas_call(
        attend_kernel,
        grid=grid,
        in_specs=[
            pl.BlockSpec(memory_space=pltpu.SMEM),
            cell_spec,
            cell_spec,
            cell_spec,
            full(w_qkv.shape),
            full(w_out.shape),
        ],
        out_specs=out_spec,
        out_shape=jax.ShapeDtypeStruct((frames, count, chans), jnp.bfloat16),
    )(valid, prev, own, nxt, w_qkv, w_out)


def shift(x, axis, step):
    count = lax.axis_size(axis)
    if step > 0:
        pairs = [(i, i + 1) for i in range(count - 1)]
    else:
        pairs = [(i + 1, i) for i in range(count - 1)]
    return lax.ppermute(x, axis, pairs)


def body(latents, w_qkv, w_out, conv_weight):
    frames, rows, merged = latents.shape
    chans = w_out.shape[0]
    cols = merged // chans
    points = rows * cols
    x_prev = shift(latents, "tm", 1)
    x_next = shift(latents, "tm", -1)
    first = lax.axis_index("tm") * frames
    total = lax.axis_size("tm") * frames
    where_t = first + jnp.arange(6, dtype=jnp.int32) - 2
    valid = ((where_t >= 0) & (where_t < total)).astype(jnp.int32)
    cells = lambda a: a.reshape(frames, points, chans)

    x_wide = jnp.concatenate([x_prev, latents, x_next], axis=0)
    halo_top = shift(x_wide[:, rows - 1 :, :], "row", 1)
    halo_bot = shift(x_wide[:, :1, :], "row", -1)
    tall = jnp.concatenate([halo_top, x_wide, halo_bot], axis=1)
    halo_left = shift(tall[:, :, merged - chans :], "col", 1)
    halo_right = shift(tall[:, :, :chans], "col", -1)

    own_c = cells(latents)
    prev_c, next_c = cells(x_prev), cells(x_next)
    half = points // 2
    hid_a = attend(valid, prev_c, own_c, next_c, w_qkv, w_out, 0, half)
    hid_b = attend(valid, prev_c, own_c, next_c, w_qkv, w_out, half, half)
    hid = jnp.concatenate([hid_a, hid_b], axis=1).reshape(frames, rows, merged)

    span = 2 * (rows + 2) + 2 * cols
    ring_pts = -(-span // BLOCK) * BLOCK
    ring = jnp.concatenate(
        [
            halo_left,
            halo_right,
            halo_top.reshape(3 * frames, cols, chans),
            halo_bot.reshape(3 * frames, cols, chans),
            jnp.zeros((3 * frames, ring_pts - span, chans), jnp.bfloat16),
        ],
        axis=1,
    )
    ring_hid = attend(
        valid, ring[:frames], ring[frames : 2 * frames], ring[2 * frames :], w_qkv, w_out
    )
    tall_n = rows + 2
    h_left = ring_hid[:, :tall_n]
    h_right = ring_hid[:, tall_n : 2 * tall_n]
    h_top = ring_hid[:, 2 * tall_n : 2 * tall_n + cols].reshape(frames, 1, merged)
    h_bot = ring_hid[:, 2 * tall_n + cols : span].reshape(frames, 1, merged)
    h_tall = jnp.concatenate([h_top, hid, h_bot], axis=1)
    padded = jnp.concatenate([h_left, h_tall, h_right], axis=2)
    taps = jnp.tile(conv_weight, (1, cols))
    acc = hid.astype(jnp.float32)
    for tap_a in range(3):
        for tap_b in range(3):
            acc = (
                acc
                + padded[:, tap_a : tap_a + rows, tap_b * chans : tap_b * chans + merged].astype(
                    jnp.float32
                )
                * taps[3 * tap_a + tap_b]
            )
    return acc.astype(jnp.bfloat16)


def solution(mesh):
    placed = (P("tm", "row", "col"), P(), P(), P())
    return jax.shard_map(
        body, mesh=mesh, in_specs=placed, out_specs=P("tm", "row", "col"), check_vma=False
    )
```

```python
import functools

import jax
import jax.numpy as jnp
from jax import lax
from jax.experimental import pallas as pl
from jax.experimental.pallas import tpu as pltpu
from jax.sharding import PartitionSpec as P

HEAD_DIM = 64
BLOCK = 128


def layer_norm_t(cols):
    mean = jnp.mean(cols, axis=0, keepdims=True)
    cent = cols - mean
    var = jnp.mean(cent * cent, axis=0, keepdims=True)
    return (cent * lax.rsqrt(var + 1e-05)).astype(jnp.bfloat16)


def attend_kernel(valid_ref, prev_ref, own_ref, next_ref, wqkv_ref, wout_ref, out_ref):
    chans = wout_ref.shape[0]
    heads = chans // HEAD_DIM
    block = own_ref.shape[2]
    frames = [prev_ref[0], prev_ref[1], own_ref[0], own_ref[1], next_ref[0], next_ref[1]]
    normed = [layer_norm_t(f.astype(jnp.float32)) for f in frames]
    own_n = jnp.concatenate([normed[2], normed[3]], axis=1)
    qkv = jnp.dot(wqkv_ref[...], own_n, preferred_element_type=jnp.float32).astype(jnp.bfloat16)
    nb_n = jnp.concatenate([normed[0], normed[1], normed[4], normed[5]], axis=1)
    kv_nb = jnp.dot(
        wqkv_ref[chans:, :], nb_n, preferred_element_type=jnp.float32
    ).astype(jnp.bfloat16)
    keys = [None] * 6
    vals = [None] * 6
    for w, slot in ((0, 0), (1, 1), (4, 2), (5, 3)):
        keys[w] = kv_nb[:chans, slot * block : (slot + 1) * block]
        vals[w] = kv_nb[chans:, slot * block : (slot + 1) * block]
    for t in range(2):
        keys[2 + t] = qkv[chans : 2 * chans, t * block : (t + 1) * block]
        vals[2 + t] = qkv[2 * chans :, t * block : (t + 1) * block]
    outs = []
    for t in range(2):
        q = qkv[:chans, t * block : (t + 1) * block].astype(jnp.float32)
        scores = []
        for d in range(5):
            w = t + d
            prod = q * keys[w].astype(jnp.float32)
            score = jnp.sum(prod.reshape(heads, HEAD_DIM, block), axis=1)
            score = score * (HEAD_DIM ** (-0.5))
            score = jnp.where(valid_ref[w] > 0, score, jnp.float32(-1e30))
            scores.append(score)
        top = scores[0]
        for s in scores[1:]:
            top = jnp.maximum(top, s)
        expo = [jnp.exp(s - top) for s in scores]
        denom = expo[0]
        for e in expo[1:]:
            denom = denom + e
        mixed = None
        for d in range(5):
            weight = (expo[d] / denom).astype(jnp.bfloat16).astype(jnp.float32)
            wide = jnp.broadcast_to(weight[:, None, :], (heads, HEAD_DIM, block)).reshape(chans, block)
            term = wide * vals[t + d].astype(jnp.float32)
            mixed = term if mixed is None else mixed + term
        outs.append(mixed.astype(jnp.bfloat16))
    attended = jnp.concatenate(outs, axis=1)
    proj = jnp.dot(wout_ref[...], attended, preferred_element_type=jnp.float32)
    xown = jnp.concatenate([own_ref[0], own_ref[1]], axis=1).astype(jnp.float32)
    hidden = (xown + proj).astype(jnp.bfloat16)
    out_ref[0] = hidden[:, :block]
    out_ref[1] = hidden[:, block:]


def attend(valid, prev, own, nxt, w_qkv, w_out):
    frames, chans, points = own.shape
    grid = (points // BLOCK,)
    assert points % BLOCK == 0
    cell_spec = pl.BlockSpec((frames, chans, BLOCK), lambda i: (0, 0, i))
    full = lambda shape: pl.BlockSpec(shape, lambda i: (0, 0))
    w_qkv = w_qkv.T
    w_out = w_out.T
    return pl.pallas_call(
        attend_kernel,
        grid=grid,
        in_specs=[
            pl.BlockSpec(memory_space=pltpu.SMEM),
            cell_spec,
            cell_spec,
            cell_spec,
            full(w_qkv.shape),
            full(w_out.shape),
        ],
        out_specs=cell_spec,
        out_shape=jax.ShapeDtypeStruct(own.shape, jnp.bfloat16),
    )(valid, prev, own, nxt, w_qkv, w_out)


def shift(x, axis, step):
    count = lax.axis_size(axis)
    if step > 0:
        pairs = [(i, i + 1) for i in range(count - 1)]
    else:
        pairs = [(i + 1, i) for i in range(count - 1)]
    return lax.ppermute(x, axis, pairs)


def body(latents, w_qkv, w_out, conv_weight):
    frames, rows, merged = latents.shape
    chans = w_out.shape[0]
    cols = merged // chans
    points = rows * cols
    x_prev = shift(latents, "tm", 1)
    x_next = shift(latents, "tm", -1)
    first = lax.axis_index("tm") * frames
    total = lax.axis_size("tm") * frames
    where_t = first + jnp.arange(6, dtype=jnp.int32) - 2
    valid = ((where_t >= 0) & (where_t < total)).astype(jnp.int32)
    cells = lambda a: a.reshape(frames, rows, cols, chans).transpose(0, 3, 1, 2).reshape(
        frames, chans, points
    )
    hidden = attend(valid, cells(x_prev), cells(latents), cells(x_next), w_qkv, w_out)
    hid = (
        hidden.reshape(frames, chans, rows, cols).transpose(0, 2, 3, 1).reshape(frames, rows, merged)
    )

    halo_top = shift(hid[:, rows - 1 :, :], "row", 1)
    halo_bot = shift(hid[:, :1, :], "row", -1)
    tall = jnp.concatenate([halo_top, hid, halo_bot], axis=1)
    halo_left = shift(tall[:, :, merged - chans :], "col", 1)
    halo_right = shift(tall[:, :, :chans], "col", -1)
    padded = jnp.concatenate([halo_left, tall, halo_right], axis=2)
    taps = jnp.tile(conv_weight, (1, cols))
    acc = hid.astype(jnp.float32)
    for tap_a in range(3):
        for tap_b in range(3):
            acc = (
                acc
                + padded[:, tap_a : tap_a + rows, tap_b * chans : tap_b * chans + merged].astype(
                    jnp.float32
                )
                * taps[3 * tap_a + tap_b]
            )
    return acc.astype(jnp.bfloat16)


def solution(mesh):
    placed = (P("tm", "row", "col"), P(), P(), P())
    return jax.shard_map(
        body, mesh=mesh, in_specs=placed, out_specs=P("tm", "row", "col"), check_vma=False
    )
```

```python
import functools

import jax
import jax.numpy as jnp
from jax import lax
from jax.experimental import pallas as pl
from jax.experimental.pallas import tpu as pltpu
from jax.sharding import PartitionSpec as P

HEAD_DIM = 64
BLOCK = 128


def layer_norm_t(cols):
    mean = jnp.mean(cols, axis=0, keepdims=True)
    cent = cols - mean
    var = jnp.mean(cent * cent, axis=0, keepdims=True)
    return (cent * lax.rsqrt(var + 1e-05)).astype(jnp.bfloat16)


def attend_kernel(valid_ref, prev_ref, own_ref, next_ref, wqkv_ref, wout_ref, out_ref):
    chans = wout_ref.shape[0]
    heads = chans // HEAD_DIM
    block = own_ref.shape[2]
    frames = [prev_ref[0], prev_ref[1], own_ref[0], own_ref[1], next_ref[0], next_ref[1]]
    normed = [layer_norm_t(f.astype(jnp.float32)) for f in frames]
    own_n = jnp.concatenate([normed[2], normed[3]], axis=1)
    qkv = jnp.dot(wqkv_ref[...], own_n, preferred_element_type=jnp.float32).astype(jnp.bfloat16)
    nb_n = jnp.concatenate([normed[0], normed[1], normed[4], normed[5]], axis=1)
    kv_nb = jnp.dot(
        wqkv_ref[chans:, :], nb_n, preferred_element_type=jnp.float32
    ).astype(jnp.bfloat16)
    keys = [None] * 6
    vals = [None] * 6
    for w, slot in ((0, 0), (1, 1), (4, 2), (5, 3)):
        keys[w] = kv_nb[:chans, slot * block : (slot + 1) * block]
        vals[w] = kv_nb[chans:, slot * block : (slot + 1) * block]
    for t in range(2):
        keys[2 + t] = qkv[chans : 2 * chans, t * block : (t + 1) * block]
        vals[2 + t] = qkv[2 * chans :, t * block : (t + 1) * block]
    outs = []
    for t in range(2):
        q = qkv[:chans, t * block : (t + 1) * block].astype(jnp.float32)
        scores = []
        for d in range(5):
            w = t + d
            prod = q * keys[w].astype(jnp.float32)
            score = jnp.sum(prod.reshape(heads, HEAD_DIM, block), axis=1)
            score = score * (HEAD_DIM ** (-0.5))
            score = jnp.where(valid_ref[w] > 0, score, jnp.float32(-1e30))
            scores.append(score)
        top = scores[0]
        for s in scores[1:]:
            top = jnp.maximum(top, s)
        expo = [jnp.exp(s - top) for s in scores]
        denom = expo[0]
        for e in expo[1:]:
            denom = denom + e
        mixed = None
        for d in range(5):
            weight = (expo[d] / denom).astype(jnp.bfloat16).astype(jnp.float32)
            wide = jnp.broadcast_to(weight[:, None, :], (heads, HEAD_DIM, block)).reshape(chans, block)
            term = wide * vals[t + d].astype(jnp.float32)
            mixed = term if mixed is None else mixed + term
        outs.append(mixed.astype(jnp.bfloat16))
    attended = jnp.concatenate(outs, axis=1)
    proj = jnp.dot(wout_ref[...], attended, preferred_element_type=jnp.float32)
    xown = jnp.concatenate([own_ref[0], own_ref[1]], axis=1).astype(jnp.float32)
    hidden = (xown + proj).astype(jnp.bfloat16)
    out_ref[0] = hidden[:, :block]
    out_ref[1] = hidden[:, block:]


def attend(valid, prev, own, nxt, w_qkv, w_out):
    frames, chans, points = own.shape
    grid = (points // BLOCK,)
    assert points % BLOCK == 0
    cell_spec = pl.BlockSpec((frames, chans, BLOCK), lambda i: (0, 0, i))
    full = lambda shape: pl.BlockSpec(shape, lambda i: (0, 0))
    w_qkv = w_qkv.T
    w_out = w_out.T
    return pl.pallas_call(
        attend_kernel,
        grid=grid,
        in_specs=[
            pl.BlockSpec(memory_space=pltpu.SMEM),
            cell_spec,
            cell_spec,
            cell_spec,
            full(w_qkv.shape),
            full(w_out.shape),
        ],
        out_specs=cell_spec,
        out_shape=jax.ShapeDtypeStruct(own.shape, jnp.bfloat16),
    )(valid, prev, own, nxt, w_qkv, w_out)


def shift(x, axis, step):
    count = lax.axis_size(axis)
    if step > 0:
        pairs = [(i, i + 1) for i in range(count - 1)]
    else:
        pairs = [(i + 1, i) for i in range(count - 1)]
    return lax.ppermute(x, axis, pairs)


def swap(send_even, send_odd, axis, offset):
    count = lax.axis_size(axis)
    pairs = []
    for i in range(offset, count - 1, 2):
        pairs += [(i, i + 1), (i + 1, i)]
    even = lax.axis_index(axis) % 2 == 0
    if offset:
        payload = jnp.where(even, send_odd, send_even)
    else:
        payload = jnp.where(even, send_even, send_odd)
    return lax.ppermute(payload, axis, pairs)


def exchange(to_next, to_prev, axis):
    even = lax.axis_index(axis) % 2 == 0
    got_a = swap(to_next, to_prev, axis, 0)
    if lax.axis_size(axis) <= 2:
        zero = jnp.zeros_like(got_a)
        return jnp.where(even, zero, got_a), jnp.where(even, got_a, zero)
    got_b = swap(to_next, to_prev, axis, 1)
    from_prev = jnp.where(even, got_b, got_a)
    from_next = jnp.where(even, got_a, got_b)
    return from_prev, from_next


def body(latents, w_qkv, w_out, conv_weight):
    frames, rows, merged = latents.shape
    chans = w_out.shape[0]
    cols = merged // chans
    points = rows * cols
    x_prev, x_next = exchange(latents, latents, "tm")
    first = lax.axis_index("tm") * frames
    total = lax.axis_size("tm") * frames
    where_t = first + jnp.arange(6, dtype=jnp.int32) - 2
    valid = ((where_t >= 0) & (where_t < total)).astype(jnp.int32)
    cells = lambda a: a.reshape(frames, rows, cols, chans).transpose(0, 3, 1, 2).reshape(
        frames, chans, points
    )
    hidden = attend(valid, cells(x_prev), cells(latents), cells(x_next), w_qkv, w_out)
    hid = (
        hidden.reshape(frames, chans, rows, cols).transpose(0, 2, 3, 1).reshape(frames, rows, merged)
    )

    halo_top, halo_bot = exchange(hid[:, rows - 1 :, :], hid[:, :1, :], "row")
    tall = jnp.concatenate([halo_top, hid, halo_bot], axis=1)
    halo_left, halo_right = exchange(tall[:, :, merged - chans :], tall[:, :, :chans], "col")
    padded = jnp.concatenate([halo_left, tall, halo_right], axis=2)
    taps = jnp.tile(conv_weight, (1, cols))
    acc = hid.astype(jnp.float32)
    for tap_a in range(3):
        for tap_b in range(3):
            acc = (
                acc
                + padded[:, tap_a : tap_a + rows, tap_b * chans : tap_b * chans + merged].astype(
                    jnp.float32
                )
                * taps[3 * tap_a + tap_b]
            )
    return acc.astype(jnp.bfloat16)


def solution(mesh):
    placed = (P("tm", "row", "col"), P(), P(), P())
    return jax.shard_map(
        body, mesh=mesh, in_specs=placed, out_specs=P("tm", "row", "col"), check_vma=False
    )
```

```python
import functools

import jax
import jax.numpy as jnp
from jax import lax
from jax.experimental import pallas as pl
from jax.experimental.pallas import tpu as pltpu
from jax.sharding import PartitionSpec as P

HEAD_DIM = 64
BLOCK = 512


def layer_norm_t(cols):
    mean = jnp.mean(cols, axis=0, keepdims=True)
    cent = cols - mean
    var = jnp.mean(cent * cent, axis=0, keepdims=True)
    return (cent * lax.rsqrt(var + 1e-05)).astype(jnp.bfloat16)


def attend_kernel(valid_ref, prev_ref, own_ref, next_ref, wqkv_ref, wout_ref, out_ref):
    chans = wout_ref.shape[0]
    heads = chans // HEAD_DIM
    block = own_ref.shape[2]
    frames = [prev_ref[0], prev_ref[1], own_ref[0], own_ref[1], next_ref[0], next_ref[1]]
    normed = [layer_norm_t(f.astype(jnp.float32)) for f in frames]
    own_n = jnp.concatenate([normed[2], normed[3]], axis=1)
    qkv = jnp.dot(wqkv_ref[...], own_n, preferred_element_type=jnp.float32).astype(jnp.bfloat16)
    nb_n = jnp.concatenate([normed[0], normed[1], normed[4], normed[5]], axis=1)
    kv_nb = jnp.dot(
        wqkv_ref[chans:, :], nb_n, preferred_element_type=jnp.float32
    ).astype(jnp.bfloat16)
    keys = [None] * 6
    vals = [None] * 6
    for w, slot in ((0, 0), (1, 1), (4, 2), (5, 3)):
        keys[w] = kv_nb[:chans, slot * block : (slot + 1) * block]
        vals[w] = kv_nb[chans:, slot * block : (slot + 1) * block]
    for t in range(2):
        keys[2 + t] = qkv[chans : 2 * chans, t * block : (t + 1) * block]
        vals[2 + t] = qkv[2 * chans :, t * block : (t + 1) * block]
    outs = []
    for t in range(2):
        q = qkv[:chans, t * block : (t + 1) * block].astype(jnp.float32)
        scores = []
        for d in range(5):
            w = t + d
            prod = q * keys[w].astype(jnp.float32)
            score = jnp.sum(prod.reshape(heads, HEAD_DIM, block), axis=1)
            score = score * (HEAD_DIM ** (-0.5))
            score = jnp.where(valid_ref[w] > 0, score, jnp.float32(-1e30))
            scores.append(score)
        top = scores[0]
        for s in scores[1:]:
            top = jnp.maximum(top, s)
        expo = [jnp.exp(s - top) for s in scores]
        denom = expo[0]
        for e in expo[1:]:
            denom = denom + e
        mixed = None
        for d in range(5):
            weight = (expo[d] / denom).astype(jnp.bfloat16).astype(jnp.float32)
            wide = jnp.broadcast_to(weight[:, None, :], (heads, HEAD_DIM, block)).reshape(chans, block)
            term = wide * vals[t + d].astype(jnp.float32)
            mixed = term if mixed is None else mixed + term
        outs.append(mixed.astype(jnp.bfloat16))
    attended = jnp.concatenate(outs, axis=1)
    proj = jnp.dot(wout_ref[...], attended, preferred_element_type=jnp.float32)
    xown = jnp.concatenate([own_ref[0], own_ref[1]], axis=1).astype(jnp.float32)
    hidden = (xown + proj).astype(jnp.bfloat16)
    out_ref[0] = hidden[:, :block]
    out_ref[1] = hidden[:, block:]


def attend(valid, prev, own, nxt, w_qkv, w_out):
    frames, chans, points = own.shape
    grid = (points // BLOCK,)
    assert points % BLOCK == 0
    cell_spec = pl.BlockSpec((frames, chans, BLOCK), lambda i: (0, 0, i))
    full = lambda shape: pl.BlockSpec(shape, lambda i: (0, 0))
    w_qkv = w_qkv.T
    w_out = w_out.T
    return pl.pallas_call(
        attend_kernel,
        grid=grid,
        in_specs=[
            pl.BlockSpec(memory_space=pltpu.SMEM),
            cell_spec,
            cell_spec,
            cell_spec,
            full(w_qkv.shape),
            full(w_out.shape),
        ],
        out_specs=cell_spec,
        out_shape=jax.ShapeDtypeStruct(own.shape, jnp.bfloat16),
    )(valid, prev, own, nxt, w_qkv, w_out)


def shift(x, axis, step):
    count = lax.axis_size(axis)
    if step > 0:
        pairs = [(i, i + 1) for i in range(count - 1)]
    else:
        pairs = [(i + 1, i) for i in range(count - 1)]
    return lax.ppermute(x, axis, pairs)


def swap(send_even, send_odd, axis, offset):
    count = lax.axis_size(axis)
    pairs = []
    for i in range(offset, count - 1, 2):
        pairs += [(i, i + 1), (i + 1, i)]
    even = lax.axis_index(axis) % 2 == 0
    if offset:
        payload = jnp.where(even, send_odd, send_even)
    else:
        payload = jnp.where(even, send_even, send_odd)
    return lax.ppermute(payload, axis, pairs)


def diag_swap(to_right, to_left, offset):
    rows = lax.axis_size("row")
    cols = lax.axis_size("col")
    pairs = []
    for c in range(offset, cols - 1, 2):
        for r in range(rows):
            pairs += [(r * cols + c, (rows - 1 - r) * cols + c + 1)]
            pairs += [((rows - 1 - r) * cols + c + 1, r * cols + c)]
    left_member = lax.axis_index("col") % 2 == offset
    payload = jnp.where(left_member, to_right, to_left)
    return lax.ppermute(payload, ("row", "col"), pairs)


def exchange(to_next, to_prev, axis):
    even = lax.axis_index(axis) % 2 == 0
    got_a = swap(to_next, to_prev, axis, 0)
    if lax.axis_size(axis) <= 2:
        zero = jnp.zeros_like(got_a)
        return jnp.where(even, zero, got_a), jnp.where(even, got_a, zero)
    got_b = swap(to_next, to_prev, axis, 1)
    from_prev = jnp.where(even, got_b, got_a)
    from_next = jnp.where(even, got_a, got_b)
    return from_prev, from_next


def body(latents, w_qkv, w_out, conv_weight):
    frames, rows, merged = latents.shape
    chans = w_out.shape[0]
    cols = merged // chans
    points = rows * cols
    x_prev, x_next = exchange(latents, latents, "tm")
    first = lax.axis_index("tm") * frames
    total = lax.axis_size("tm") * frames
    where_t = first + jnp.arange(6, dtype=jnp.int32) - 2
    valid = ((where_t >= 0) & (where_t < total)).astype(jnp.int32)
    cells = lambda a: a.reshape(frames, rows, cols, chans).transpose(0, 3, 1, 2).reshape(
        frames, chans, points
    )
    hidden = attend(valid, cells(x_prev), cells(latents), cells(x_next), w_qkv, w_out)
    hid = (
        hidden.reshape(frames, chans, rows, cols).transpose(0, 2, 3, 1).reshape(frames, rows, merged)
    )

    bot_row = hid[:, rows - 1 :, :]
    top_row = hid[:, :1, :]
    halo_top, halo_bot = exchange(bot_row, top_row, "row")
    halo_left, halo_right = exchange(hid[:, :, merged - chans :], hid[:, :, :chans], "col")
    upper = lax.axis_index("row") == 0
    to_right = jnp.where(upper, bot_row[:, :, merged - chans :], top_row[:, :, merged - chans :])
    to_left = jnp.where(upper, bot_row[:, :, :chans], top_row[:, :, :chans])
    got_a = diag_swap(to_right, to_left, 0)
    got_b = diag_swap(to_right, to_left, 1)
    even = lax.axis_index("col") % 2 == 0
    from_right = jnp.where(even, got_a, got_b)
    from_left = jnp.where(even, got_b, got_a)
    zero = jnp.zeros_like(from_left)
    c_tl = jnp.where(upper, zero, from_left)
    c_bl = jnp.where(upper, from_left, zero)
    c_tr = jnp.where(upper, zero, from_right)
    c_br = jnp.where(upper, from_right, zero)
    padded = jnp.concatenate(
        [
            jnp.concatenate([c_tl, halo_top, c_tr], axis=2),
            jnp.concatenate([halo_left, hid, halo_right], axis=2),
            jnp.concatenate([c_bl, halo_bot, c_br], axis=2),
        ],
        axis=1,
    )
    taps = jnp.tile(conv_weight, (1, cols))
    acc = hid.astype(jnp.float32)
    for tap_a in range(3):
        for tap_b in range(3):
            acc = (
                acc
                + padded[:, tap_a : tap_a + rows, tap_b * chans : tap_b * chans + merged].astype(
                    jnp.float32
                )
                * taps[3 * tap_a + tap_b]
            )
    return acc.astype(jnp.bfloat16)


def solution(mesh):
    placed = (P("tm", "row", "col"), P(), P(), P())
    return jax.shard_map(
        body, mesh=mesh, in_specs=placed, out_specs=P("tm", "row", "col"), check_vma=False
    )
```

```python
import functools

import jax
import jax.numpy as jnp
from jax import lax
from jax.experimental import pallas as pl
from jax.experimental.pallas import tpu as pltpu
from jax.sharding import PartitionSpec as P

HEAD_DIM = 64
BLOCK = 512


def layer_norm_t(cols):
    mean = jnp.mean(cols, axis=0, keepdims=True)
    cent = cols - mean
    var = jnp.mean(cent * cent, axis=0, keepdims=True)
    return (cent * lax.rsqrt(var + 1e-05)).astype(jnp.bfloat16)


def attend_kernel(valid_ref, prev_ref, own_ref, next_ref, wqkv_ref, wout_ref, out_ref):
    chans = wout_ref.shape[0]
    heads = chans // HEAD_DIM
    block = own_ref.shape[2]
    frames = [prev_ref[0], prev_ref[1], own_ref[0], own_ref[1], next_ref[0], next_ref[1]]
    normed = [layer_norm_t(f.astype(jnp.float32)) for f in frames]
    own_n = jnp.concatenate([normed[2], normed[3]], axis=1)
    qkv = jnp.dot(wqkv_ref[...], own_n, preferred_element_type=jnp.float32).astype(jnp.bfloat16)
    nb_n = jnp.concatenate([normed[0], normed[1], normed[4], normed[5]], axis=1)
    kv_nb = jnp.dot(
        wqkv_ref[chans:, :], nb_n, preferred_element_type=jnp.float32
    ).astype(jnp.bfloat16)
    keys = [None] * 6
    vals = [None] * 6
    for w, slot in ((0, 0), (1, 1), (4, 2), (5, 3)):
        keys[w] = kv_nb[:chans, slot * block : (slot + 1) * block]
        vals[w] = kv_nb[chans:, slot * block : (slot + 1) * block]
    for t in range(2):
        keys[2 + t] = qkv[chans : 2 * chans, t * block : (t + 1) * block]
        vals[2 + t] = qkv[2 * chans :, t * block : (t + 1) * block]
    outs = []
    for t in range(2):
        q = qkv[:chans, t * block : (t + 1) * block].astype(jnp.float32)
        scores = []
        for d in range(5):
            w = t + d
            prod = q * keys[w].astype(jnp.float32)
            score = jnp.sum(prod.reshape(heads, HEAD_DIM, block), axis=1)
            score = score * (HEAD_DIM ** (-0.5))
            score = jnp.where(valid_ref[w] > 0, score, jnp.float32(-1e30))
            scores.append(score)
        top = scores[0]
        for s in scores[1:]:
            top = jnp.maximum(top, s)
        expo = [jnp.exp(s - top) for s in scores]
        denom = expo[0]
        for e in expo[1:]:
            denom = denom + e
        mixed = None
        for d in range(5):
            weight = (expo[d] / denom).astype(jnp.bfloat16).astype(jnp.float32)
            wide = jnp.broadcast_to(weight[:, None, :], (heads, HEAD_DIM, block)).reshape(chans, block)
            term = wide * vals[t + d].astype(jnp.float32)
            mixed = term if mixed is None else mixed + term
        outs.append(mixed.astype(jnp.bfloat16))
    attended = jnp.concatenate(outs, axis=1)
    proj = jnp.dot(wout_ref[...], attended, preferred_element_type=jnp.float32)
    xown = jnp.concatenate([own_ref[0], own_ref[1]], axis=1).astype(jnp.float32)
    hidden = (xown + proj).astype(jnp.bfloat16)
    out_ref[0] = hidden[:, :block]
    out_ref[1] = hidden[:, block:]


def attend(valid, prev, own, nxt, w_qkv, w_out):
    frames, chans, points = own.shape
    grid = (points // BLOCK,)
    assert points % BLOCK == 0
    cell_spec = pl.BlockSpec((frames, chans, BLOCK), lambda i: (0, 0, i))
    full = lambda shape: pl.BlockSpec(shape, lambda i: (0, 0))
    w_qkv = w_qkv.T
    w_out = w_out.T
    return pl.pallas_call(
        attend_kernel,
        grid=grid,
        in_specs=[
            pl.BlockSpec(memory_space=pltpu.SMEM),
            cell_spec,
            cell_spec,
            cell_spec,
            full(w_qkv.shape),
            full(w_out.shape),
        ],
        out_specs=cell_spec,
        out_shape=jax.ShapeDtypeStruct(own.shape, jnp.bfloat16),
    )(valid, prev, own, nxt, w_qkv, w_out)


def shift(x, axis, step):
    count = lax.axis_size(axis)
    if step > 0:
        pairs = [(i, i + 1) for i in range(count - 1)]
    else:
        pairs = [(i + 1, i) for i in range(count - 1)]
    return lax.ppermute(x, axis, pairs)


def swap(send_even, send_odd, axis, offset):
    count = lax.axis_size(axis)
    pairs = []
    for i in range(offset, count - 1, 2):
        pairs += [(i, i + 1), (i + 1, i)]
    even = lax.axis_index(axis) % 2 == 0
    if offset:
        payload = jnp.where(even, send_odd, send_even)
    else:
        payload = jnp.where(even, send_even, send_odd)
    return lax.ppermute(payload, axis, pairs)


def exchange(to_next, to_prev, axis):
    even = lax.axis_index(axis) % 2 == 0
    got_a = swap(to_next, to_prev, axis, 0)
    if lax.axis_size(axis) <= 2:
        zero = jnp.zeros_like(got_a)
        return jnp.where(even, zero, got_a), jnp.where(even, got_a, zero)
    got_b = swap(to_next, to_prev, axis, 1)
    from_prev = jnp.where(even, got_b, got_a)
    from_next = jnp.where(even, got_a, got_b)
    return from_prev, from_next


def body(latents, w_qkv, w_out, conv_weight):
    frames, rows, merged = latents.shape
    chans = w_out.shape[0]
    cols = merged // chans
    points = rows * cols
    x_prev, x_next = exchange(latents, latents, "tm")
    first = lax.axis_index("tm") * frames
    total = lax.axis_size("tm") * frames
    where_t = first + jnp.arange(6, dtype=jnp.int32) - 2
    valid = ((where_t >= 0) & (where_t < total)).astype(jnp.int32)
    cells = lambda a: a.reshape(frames, rows, cols, chans).transpose(0, 3, 1, 2).reshape(
        frames, chans, points
    )
    hidden = attend(valid, cells(x_prev), cells(latents), cells(x_next), w_qkv, w_out)
    hid = (
        hidden.reshape(frames, chans, rows, cols).transpose(0, 2, 3, 1).reshape(frames, rows, merged)
    )

    halo_top, halo_bot = exchange(hid[:, rows - 1 :, :], hid[:, :1, :], "row")
    tall = jnp.concatenate([halo_top, hid, halo_bot], axis=1)
    halo_left, halo_right = exchange(tall[:, :, merged - chans :], tall[:, :, :chans], "col")
    padded = jnp.concatenate([halo_left, tall, halo_right], axis=2)
    taps = jnp.tile(conv_weight, (1, cols))
    acc = hid.astype(jnp.float32)
    for tap_a in range(3):
        for tap_b in range(3):
            acc = (
                acc
                + padded[:, tap_a : tap_a + rows, tap_b * chans : tap_b * chans + merged].astype(
                    jnp.float32
                )
                * taps[3 * tap_a + tap_b]
            )
    return acc.astype(jnp.bfloat16)


def solution(mesh):
    placed = (P("tm", "row", "col"), P(), P(), P())
    return jax.shard_map(
        body, mesh=mesh, in_specs=placed, out_specs=P("tm", "row", "col"), check_vma=False
    )
```

```python
import functools

import jax
import jax.numpy as jnp
from jax import lax
from jax.experimental import pallas as pl
from jax.experimental.pallas import tpu as pltpu
from jax.sharding import PartitionSpec as P

HEAD_DIM = 64
BLOCK = 512


def layer_norm_t(cols):
    mean = jnp.mean(cols, axis=0, keepdims=True)
    cent = cols - mean
    var = jnp.mean(cent * cent, axis=0, keepdims=True)
    return (cent * lax.rsqrt(var + 1e-05)).astype(jnp.bfloat16)


def attend_kernel(valid_ref, prev_ref, own_ref, next_ref, wqkv_ref, wout_ref, out_ref):
    chans = wout_ref.shape[0]
    heads = chans // HEAD_DIM
    block = own_ref.shape[2]
    frames = [prev_ref[0], prev_ref[1], own_ref[0], own_ref[1], next_ref[0], next_ref[1]]
    normed = [layer_norm_t(f.astype(jnp.float32)) for f in frames]
    own_n = jnp.concatenate([normed[2], normed[3]], axis=1)
    qkv = jnp.dot(wqkv_ref[...], own_n, preferred_element_type=jnp.float32).astype(jnp.bfloat16)
    nb_n = jnp.concatenate([normed[0], normed[1], normed[4], normed[5]], axis=1)
    kv_nb = jnp.dot(
        wqkv_ref[chans:, :], nb_n, preferred_element_type=jnp.float32
    ).astype(jnp.bfloat16)
    keys = [None] * 6
    vals = [None] * 6
    for w, slot in ((0, 0), (1, 1), (4, 2), (5, 3)):
        keys[w] = kv_nb[:chans, slot * block : (slot + 1) * block]
        vals[w] = kv_nb[chans:, slot * block : (slot + 1) * block]
    for t in range(2):
        keys[2 + t] = qkv[chans : 2 * chans, t * block : (t + 1) * block]
        vals[2 + t] = qkv[2 * chans :, t * block : (t + 1) * block]
    outs = []
    for t in range(2):
        q = qkv[:chans, t * block : (t + 1) * block].astype(jnp.float32)
        scores = []
        for d in range(5):
            w = t + d
            prod = q * keys[w].astype(jnp.float32)
            score = jnp.sum(prod.reshape(heads, HEAD_DIM, block), axis=1)
            score = score * (HEAD_DIM ** (-0.5))
            score = jnp.where(valid_ref[w] > 0, score, jnp.float32(-1e30))
            scores.append(score)
        top = scores[0]
        for s in scores[1:]:
            top = jnp.maximum(top, s)
        expo = [jnp.exp(s - top) for s in scores]
        denom = expo[0]
        for e in expo[1:]:
            denom = denom + e
        mixed = None
        for d in range(5):
            weight = (expo[d] / denom).astype(jnp.bfloat16).astype(jnp.float32)
            wide = jnp.broadcast_to(weight[:, None, :], (heads, HEAD_DIM, block)).reshape(chans, block)
            term = wide * vals[t + d].astype(jnp.float32)
            mixed = term if mixed is None else mixed + term
        outs.append(mixed.astype(jnp.bfloat16))
    attended = jnp.concatenate(outs, axis=1)
    proj = jnp.dot(wout_ref[...], attended, preferred_element_type=jnp.float32)
    xown = jnp.concatenate([own_ref[0], own_ref[1]], axis=1).astype(jnp.float32)
    hidden = (xown + proj).astype(jnp.bfloat16)
    out_ref[0] = hidden[:, :block]
    out_ref[1] = hidden[:, block:]


def attend(valid, prev, own, nxt, w_qkv, w_out):
    frames, chans, points = own.shape
    grid = (points // BLOCK,)
    assert points % BLOCK == 0
    cell_spec = pl.BlockSpec((frames, chans, BLOCK), lambda i: (0, 0, i))
    full = lambda shape: pl.BlockSpec(shape, lambda i: (0, 0))
    w_qkv = w_qkv.T
    w_out = w_out.T
    return pl.pallas_call(
        attend_kernel,
        grid=grid,
        in_specs=[
            pl.BlockSpec(memory_space=pltpu.SMEM),
            cell_spec,
            cell_spec,
            cell_spec,
            full(w_qkv.shape),
            full(w_out.shape),
        ],
        out_specs=cell_spec,
        out_shape=jax.ShapeDtypeStruct(own.shape, jnp.bfloat16),
    )(valid, prev, own, nxt, w_qkv, w_out)


def shift(x, axis, step):
    count = lax.axis_size(axis)
    if step > 0:
        pairs = [(i, i + 1) for i in range(count - 1)]
    else:
        pairs = [(i + 1, i) for i in range(count - 1)]
    return lax.ppermute(x, axis, pairs)


def swap(send_even, send_odd, axis, offset):
    count = lax.axis_size(axis)
    pairs = []
    for i in range(offset, count - 1, 2):
        pairs += [(i, i + 1), (i + 1, i)]
    even = lax.axis_index(axis) % 2 == 0
    if offset:
        payload = jnp.where(even, send_odd, send_even)
    else:
        payload = jnp.where(even, send_even, send_odd)
    return lax.ppermute(payload, axis, pairs)


def exchange(to_next, to_prev, axis):
    even = lax.axis_index(axis) % 2 == 0
    got_a = swap(to_next, to_prev, axis, 0)
    if lax.axis_size(axis) <= 2:
        zero = jnp.zeros_like(got_a)
        return jnp.where(even, zero, got_a), jnp.where(even, got_a, zero)
    got_b = swap(to_next, to_prev, axis, 1)
    from_prev = jnp.where(even, got_b, got_a)
    from_next = jnp.where(even, got_a, got_b)
    return from_prev, from_next


def body(latents, w_qkv, w_out, conv_weight):
    frames, rows, merged = latents.shape
    chans = w_out.shape[0]
    cols = merged // chans
    points = rows * cols
    cells = lambda a: a.reshape(frames, rows, cols, chans).transpose(0, 3, 1, 2).reshape(
        frames, chans, points
    )
    own_c = cells(latents)
    x_prev, x_next = exchange(own_c, own_c, "tm")
    first = lax.axis_index("tm") * frames
    total = lax.axis_size("tm") * frames
    where_t = first + jnp.arange(6, dtype=jnp.int32) - 2
    valid = ((where_t >= 0) & (where_t < total)).astype(jnp.int32)
    hidden = attend(valid, x_prev, own_c, x_next, w_qkv, w_out)
    hid = (
        hidden.reshape(frames, chans, rows, cols).transpose(0, 2, 3, 1).reshape(frames, rows, merged)
    )

    halo_top, halo_bot = exchange(hid[:, rows - 1 :, :], hid[:, :1, :], "row")
    tall = jnp.concatenate([halo_top, hid, halo_bot], axis=1)
    halo_left, halo_right = exchange(tall[:, :, merged - chans :], tall[:, :, :chans], "col")
    padded = jnp.concatenate([halo_left, tall, halo_right], axis=2)
    taps = jnp.tile(conv_weight, (1, cols))
    acc = hid.astype(jnp.float32)
    for tap_a in range(3):
        for tap_b in range(3):
            acc = (
                acc
                + padded[:, tap_a : tap_a + rows, tap_b * chans : tap_b * chans + merged].astype(
                    jnp.float32
                )
                * taps[3 * tap_a + tap_b]
            )
    return acc.astype(jnp.bfloat16)


def solution(mesh):
    placed = (P("tm", "row", "col"), P(), P(), P())
    return jax.shard_map(
        body, mesh=mesh, in_specs=placed, out_specs=P("tm", "row", "col"), check_vma=False
    )
```

```python
import functools

import jax
import jax.numpy as jnp
from jax import lax
from jax.experimental import pallas as pl
from jax.experimental.pallas import tpu as pltpu
from jax.sharding import PartitionSpec as P

HEAD_DIM = 64
BLOCK = 512


def layer_norm_t(cols):
    mean = jnp.mean(cols, axis=0, keepdims=True)
    cent = cols - mean
    var = jnp.mean(cent * cent, axis=0, keepdims=True)
    return (cent * lax.rsqrt(var + 1e-05)).astype(jnp.bfloat16)


def attend_kernel(valid_ref, prev_ref, own_ref, next_ref, wqkv_ref, wout_ref, out_ref):
    chans = wout_ref.shape[0]
    heads = chans // HEAD_DIM
    block = own_ref.shape[2]
    frames = [prev_ref[0], prev_ref[1], own_ref[0], own_ref[1], next_ref[0], next_ref[1]]
    normed = [layer_norm_t(f.astype(jnp.float32)) for f in frames]
    own_n = jnp.concatenate([normed[2], normed[3]], axis=1)
    qkv = jnp.dot(wqkv_ref[...], own_n, preferred_element_type=jnp.float32).astype(jnp.bfloat16)
    nb_n = jnp.concatenate([normed[0], normed[1], normed[4], normed[5]], axis=1)
    kv_nb = jnp.dot(
        wqkv_ref[chans:, :], nb_n, preferred_element_type=jnp.float32
    ).astype(jnp.bfloat16)
    keys = [None] * 6
    vals = [None] * 6
    for w, slot in ((0, 0), (1, 1), (4, 2), (5, 3)):
        keys[w] = kv_nb[:chans, slot * block : (slot + 1) * block]
        vals[w] = kv_nb[chans:, slot * block : (slot + 1) * block]
    for t in range(2):
        keys[2 + t] = qkv[chans : 2 * chans, t * block : (t + 1) * block]
        vals[2 + t] = qkv[2 * chans :, t * block : (t + 1) * block]
    outs = []
    for t in range(2):
        q = qkv[:chans, t * block : (t + 1) * block].astype(jnp.float32)
        scores = []
        for d in range(5):
            w = t + d
            prod = q * keys[w].astype(jnp.float32)
            score = jnp.sum(prod.reshape(heads, HEAD_DIM, block), axis=1)
            score = score * (HEAD_DIM ** (-0.5))
            score = jnp.where(valid_ref[w] > 0, score, jnp.float32(-1e30))
            scores.append(score)
        top = scores[0]
        for s in scores[1:]:
            top = jnp.maximum(top, s)
        expo = [jnp.exp(s - top) for s in scores]
        denom = expo[0]
        for e in expo[1:]:
            denom = denom + e
        mixed = None
        for d in range(5):
            weight = (expo[d] / denom).astype(jnp.bfloat16).astype(jnp.float32)
            wide = jnp.broadcast_to(weight[:, None, :], (heads, HEAD_DIM, block)).reshape(chans, block)
            term = wide * vals[t + d].astype(jnp.float32)
            mixed = term if mixed is None else mixed + term
        outs.append(mixed.astype(jnp.bfloat16))
    attended = jnp.concatenate(outs, axis=1)
    proj = jnp.dot(wout_ref[...], attended, preferred_element_type=jnp.float32)
    xown = jnp.concatenate([own_ref[0], own_ref[1]], axis=1).astype(jnp.float32)
    hidden = (xown + proj).astype(jnp.bfloat16)
    out_ref[0] = hidden[:, :block]
    out_ref[1] = hidden[:, block:]


def attend(valid, prev, own, nxt, w_qkv, w_out):
    frames, chans, points = own.shape
    grid = (points // BLOCK,)
    assert points % BLOCK == 0
    cell_spec = pl.BlockSpec((frames, chans, BLOCK), lambda i: (0, 0, i))
    full = lambda shape: pl.BlockSpec(shape, lambda i: (0, 0))
    w_qkv = w_qkv.T
    w_out = w_out.T
    return pl.pallas_call(
        attend_kernel,
        grid=grid,
        in_specs=[
            pl.BlockSpec(memory_space=pltpu.SMEM),
            cell_spec,
            cell_spec,
            cell_spec,
            full(w_qkv.shape),
            full(w_out.shape),
        ],
        out_specs=cell_spec,
        out_shape=jax.ShapeDtypeStruct(own.shape, jnp.bfloat16),
    )(valid, prev, own, nxt, w_qkv, w_out)


def shift(x, axis, step):
    count = lax.axis_size(axis)
    if step > 0:
        pairs = [(i, i + 1) for i in range(count - 1)]
    else:
        pairs = [(i + 1, i) for i in range(count - 1)]
    return lax.ppermute(x, axis, pairs)


def swap(send_even, send_odd, axis, offset):
    count = lax.axis_size(axis)
    pairs = []
    for i in range(offset, count - 1, 2):
        pairs += [(i, i + 1), (i + 1, i)]
    even = lax.axis_index(axis) % 2 == 0
    if offset:
        payload = jnp.where(even, send_odd, send_even)
    else:
        payload = jnp.where(even, send_even, send_odd)
    return lax.ppermute(payload, axis, pairs)


def exchange(to_next, to_prev, axis):
    even = lax.axis_index(axis) % 2 == 0
    got_a = swap(to_next, to_prev, axis, 0)
    if lax.axis_size(axis) <= 2:
        zero = jnp.zeros_like(got_a)
        return jnp.where(even, zero, got_a), jnp.where(even, got_a, zero)
    got_b = swap(to_next, to_prev, axis, 1)
    from_prev = jnp.where(even, got_b, got_a)
    from_next = jnp.where(even, got_a, got_b)
    return from_prev, from_next


def body(latents, w_qkv, w_out, conv_weight):
    frames, rows, merged = latents.shape
    chans = w_out.shape[0]
    cols = merged // chans
    points = rows * cols
    cells = lambda a: a.reshape(frames, rows, cols, chans).transpose(0, 3, 1, 2).reshape(
        frames, chans, points
    )
    own_c = cells(latents)
    x_prev, x_next = exchange(own_c, own_c, "tm")
    first = lax.axis_index("tm") * frames
    total = lax.axis_size("tm") * frames
    where_t = first + jnp.arange(6, dtype=jnp.int32) - 2
    valid = ((where_t >= 0) & (where_t < total)).astype(jnp.int32)
    hidden = attend(valid, x_prev, own_c, x_next, w_qkv, w_out)
    hid = (
        hidden.reshape(frames, chans, rows, cols).transpose(0, 2, 3, 1).reshape(frames, rows, merged)
    )
    as_row = lambda a: a.transpose(0, 2, 1).reshape(frames, 1, merged)
    as_col = lambda a: a.transpose(0, 2, 1)
    bot_row = as_row(hidden[:, :, (rows - 1) * cols :])
    top_row = as_row(hidden[:, :, :cols])
    halo_top, halo_bot = exchange(bot_row, top_row, "row")
    left_col = as_col(hidden[:, :, 0::cols])
    right_col = as_col(hidden[:, :, cols - 1 :: cols])
    tall_l = jnp.concatenate([halo_top[:, :, :chans], left_col, halo_bot[:, :, :chans]], axis=1)
    tall_r = jnp.concatenate(
        [halo_top[:, :, merged - chans :], right_col, halo_bot[:, :, merged - chans :]], axis=1
    )
    halo_left, halo_right = exchange(tall_r, tall_l, "col")

    taps = jnp.tile(conv_weight, (1, cols))
    zero_col = jnp.zeros((frames, rows + 2, chans), jnp.bfloat16)
    zero_row = jnp.zeros((frames, 1, merged), jnp.bfloat16)
    padded = jnp.concatenate(
        [zero_col, jnp.concatenate([zero_row, hid, zero_row], axis=1), zero_col], axis=2
    )
    acc = hid.astype(jnp.float32)
    for tap_a in range(3):
        for tap_b in range(3):
            acc = (
                acc
                + padded[:, tap_a : tap_a + rows, tap_b * chans : tap_b * chans + merged].astype(
                    jnp.float32
                )
                * taps[3 * tap_a + tap_b]
            )
    acc = lax.optimization_barrier(acc)
    top_full = jnp.concatenate([halo_left[:, :1], halo_top, halo_right[:, :1]], axis=2)
    bot_full = jnp.concatenate([halo_left[:, rows + 1 :], halo_bot, halo_right[:, rows + 1 :]], axis=2)
    row_term = lambda full, a: sum(
        full[:, :, b * chans : b * chans + merged].astype(jnp.float32) * taps[3 * a + b]
        for b in range(3)
    )
    side = lambda halo: jnp.concatenate(
        [jnp.zeros((frames, 1, chans), jnp.bfloat16), halo[:, 1 : rows + 1], jnp.zeros((frames, 1, chans), jnp.bfloat16)],
        axis=1,
    )
    col_term = lambda halo, b: sum(
        side(halo)[:, a : a + rows].astype(jnp.float32) * conv_weight[3 * a + b] for a in range(3)
    )
    border = (
        jnp.pad(row_term(top_full, 0), ((0, 0), (0, rows - 1), (0, 0)))
        + jnp.pad(row_term(bot_full, 2), ((0, 0), (rows - 1, 0), (0, 0)))
        + jnp.pad(col_term(halo_left, 0), ((0, 0), (0, 0), (0, merged - chans)))
        + jnp.pad(col_term(halo_right, 2), ((0, 0), (0, 0), (merged - chans, 0)))
    )
    acc = acc + border
    return acc.astype(jnp.bfloat16)


def solution(mesh):
    placed = (P("tm", "row", "col"), P(), P(), P())
    return jax.shard_map(
        body, mesh=mesh, in_specs=placed, out_specs=P("tm", "row", "col"), check_vma=False
    )
```

```python
import functools

import jax
import jax.numpy as jnp
from jax import lax
from jax.experimental import pallas as pl
from jax.experimental.pallas import tpu as pltpu
from jax.sharding import PartitionSpec as P

HEAD_DIM = 64
BLOCK = 512


def layer_norm_t(cols):
    mean = jnp.mean(cols, axis=0, keepdims=True)
    cent = cols - mean
    var = jnp.mean(cent * cent, axis=0, keepdims=True)
    return (cent * lax.rsqrt(var + 1e-05)).astype(jnp.bfloat16)


def attend_kernel(valid_ref, a_ref, own_ref, b_ref, wqkv_ref, wout_ref, out_ref):
    @pl.when(valid_ref[6] > 0)
    def _():
        attend_body(valid_ref, b_ref, own_ref, a_ref, wqkv_ref, wout_ref, out_ref)

    @pl.when(valid_ref[6] == 0)
    def _():
        attend_body(valid_ref, a_ref, own_ref, b_ref, wqkv_ref, wout_ref, out_ref)


def attend_body(valid_ref, prev_ref, own_ref, next_ref, wqkv_ref, wout_ref, out_ref):
    chans = wout_ref.shape[0]
    heads = chans // HEAD_DIM
    block = own_ref.shape[2]
    frames = [prev_ref[0], prev_ref[1], own_ref[0], own_ref[1], next_ref[0], next_ref[1]]
    normed = [layer_norm_t(f.astype(jnp.float32)) for f in frames]
    own_n = jnp.concatenate([normed[2], normed[3]], axis=1)
    qkv = jnp.dot(wqkv_ref[...], own_n, preferred_element_type=jnp.float32).astype(jnp.bfloat16)
    nb_n = jnp.concatenate([normed[0], normed[1], normed[4], normed[5]], axis=1)
    kv_nb = jnp.dot(
        wqkv_ref[chans:, :], nb_n, preferred_element_type=jnp.float32
    ).astype(jnp.bfloat16)
    keys = [None] * 6
    vals = [None] * 6
    for w, slot in ((0, 0), (1, 1), (4, 2), (5, 3)):
        keys[w] = kv_nb[:chans, slot * block : (slot + 1) * block]
        vals[w] = kv_nb[chans:, slot * block : (slot + 1) * block]
    for t in range(2):
        keys[2 + t] = qkv[chans : 2 * chans, t * block : (t + 1) * block]
        vals[2 + t] = qkv[2 * chans :, t * block : (t + 1) * block]
    outs = []
    for t in range(2):
        q = qkv[:chans, t * block : (t + 1) * block].astype(jnp.float32)
        scores = []
        for d in range(5):
            w = t + d
            prod = q * keys[w].astype(jnp.float32)
            score = jnp.sum(prod.reshape(heads, HEAD_DIM, block), axis=1)
            score = score * (HEAD_DIM ** (-0.5))
            score = jnp.where(valid_ref[w] > 0, score, jnp.float32(-1e30))
            scores.append(score)
        top = scores[0]
        for s in scores[1:]:
            top = jnp.maximum(top, s)
        expo = [jnp.exp(s - top) for s in scores]
        denom = expo[0]
        for e in expo[1:]:
            denom = denom + e
        mixed = None
        for d in range(5):
            weight = (expo[d] / denom).astype(jnp.bfloat16).astype(jnp.float32)
            wide = jnp.broadcast_to(weight[:, None, :], (heads, HEAD_DIM, block)).reshape(chans, block)
            term = wide * vals[t + d].astype(jnp.float32)
            mixed = term if mixed is None else mixed + term
        outs.append(mixed.astype(jnp.bfloat16))
    attended = jnp.concatenate(outs, axis=1)
    proj = jnp.dot(wout_ref[...], attended, preferred_element_type=jnp.float32)
    xown = jnp.concatenate([own_ref[0], own_ref[1]], axis=1).astype(jnp.float32)
    hidden = (xown + proj).astype(jnp.bfloat16)
    out_ref[0] = hidden[:, :block]
    out_ref[1] = hidden[:, block:]


def attend(valid, prev, own, nxt, w_qkv, w_out):
    frames, chans, points = own.shape
    grid = (points // BLOCK,)
    assert points % BLOCK == 0
    cell_spec = pl.BlockSpec((frames, chans, BLOCK), lambda i: (0, 0, i))
    full = lambda shape: pl.BlockSpec(shape, lambda i: (0, 0))
    w_qkv = w_qkv.T
    w_out = w_out.T
    return pl.pallas_call(
        attend_kernel,
        grid=grid,
        in_specs=[
            pl.BlockSpec(memory_space=pltpu.SMEM),
            cell_spec,
            cell_spec,
            cell_spec,
            full(w_qkv.shape),
            full(w_out.shape),
        ],
        out_specs=cell_spec,
        out_shape=jax.ShapeDtypeStruct(own.shape, jnp.bfloat16),
    )(valid, prev, own, nxt, w_qkv, w_out)


def shift(x, axis, step):
    count = lax.axis_size(axis)
    if step > 0:
        pairs = [(i, i + 1) for i in range(count - 1)]
    else:
        pairs = [(i + 1, i) for i in range(count - 1)]
    return lax.ppermute(x, axis, pairs)


def swap(send_even, send_odd, axis, offset):
    count = lax.axis_size(axis)
    pairs = []
    for i in range(offset, count - 1, 2):
        pairs += [(i, i + 1), (i + 1, i)]
    even = lax.axis_index(axis) % 2 == 0
    if offset:
        payload = jnp.where(even, send_odd, send_even)
    else:
        payload = jnp.where(even, send_even, send_odd)
    return lax.ppermute(payload, axis, pairs)


def exchange(to_next, to_prev, axis):
    even = lax.axis_index(axis) % 2 == 0
    got_a = swap(to_next, to_prev, axis, 0)
    if lax.axis_size(axis) <= 2:
        zero = jnp.zeros_like(got_a)
        return jnp.where(even, zero, got_a), jnp.where(even, got_a, zero)
    got_b = swap(to_next, to_prev, axis, 1)
    from_prev = jnp.where(even, got_b, got_a)
    from_next = jnp.where(even, got_a, got_b)
    return from_prev, from_next


def body(latents, w_qkv, w_out, conv_weight):
    frames, rows, merged = latents.shape
    chans = w_out.shape[0]
    cols = merged // chans
    points = rows * cols
    cells = lambda a: a.reshape(frames, rows, cols, chans).transpose(0, 3, 1, 2).reshape(
        frames, chans, points
    )
    own_c = cells(latents)
    got_a = swap(own_c, own_c, "tm", 0)
    got_b = swap(own_c, own_c, "tm", 1)
    first = lax.axis_index("tm") * frames
    total = lax.axis_size("tm") * frames
    where_t = first + jnp.arange(6, dtype=jnp.int32) - 2
    valid = ((where_t >= 0) & (where_t < total)).astype(jnp.int32)
    even = (lax.axis_index("tm") % 2 == 0).astype(jnp.int32)
    valid = jnp.concatenate([valid, even[None]])
    hidden = attend(valid, got_a, own_c, got_b, w_qkv, w_out)
    hid = (
        hidden.reshape(frames, chans, rows, cols).transpose(0, 2, 3, 1).reshape(frames, rows, merged)
    )

    halo_top, halo_bot = exchange(hid[:, rows - 1 :, :], hid[:, :1, :], "row")
    tall = jnp.concatenate([halo_top, hid, halo_bot], axis=1)
    halo_left, halo_right = exchange(tall[:, :, merged - chans :], tall[:, :, :chans], "col")
    padded = jnp.concatenate([halo_left, tall, halo_right], axis=2)
    taps = jnp.tile(conv_weight, (1, cols))
    acc = hid.astype(jnp.float32)
    for tap_a in range(3):
        for tap_b in range(3):
            acc = (
                acc
                + padded[:, tap_a : tap_a + rows, tap_b * chans : tap_b * chans + merged].astype(
                    jnp.float32
                )
                * taps[3 * tap_a + tap_b]
            )
    return acc.astype(jnp.bfloat16)


def solution(mesh):
    placed = (P("tm", "row", "col"), P(), P(), P())
    return jax.shard_map(
        body, mesh=mesh, in_specs=placed, out_specs=P("tm", "row", "col"), check_vma=False
    )
```

```python
import functools

import jax
import jax.numpy as jnp
from jax import lax
from jax.experimental import pallas as pl
from jax.experimental.pallas import tpu as pltpu
from jax.sharding import PartitionSpec as P

HEAD_DIM = 64
BLOCK = 512


def layer_norm_t(cols):
    mean = jnp.mean(cols, axis=0, keepdims=True)
    cent = cols - mean
    var = jnp.mean(cent * cent, axis=0, keepdims=True)
    return (cent * lax.rsqrt(var + 1e-05)).astype(jnp.bfloat16)


def attend_kernel(valid_ref, a_ref, own_ref, b0_ref, b1_ref, wqkv_ref, wout_ref, out_ref):
    near = [a_ref.at[0], a_ref.at[1]]
    far = [b0_ref.at[0], b1_ref.at[0]]

    @pl.when(valid_ref[6] > 0)
    def _():
        attend_body(valid_ref, far, own_ref, near, wqkv_ref, wout_ref, out_ref)

    @pl.when(valid_ref[6] == 0)
    def _():
        attend_body(valid_ref, near, own_ref, far, wqkv_ref, wout_ref, out_ref)


def attend_body(valid_ref, prev_refs, own_ref, next_refs, wqkv_ref, wout_ref, out_ref):
    chans = wout_ref.shape[0]
    heads = chans // HEAD_DIM
    block = own_ref.shape[2]
    frames = [prev_refs[0][...], prev_refs[1][...], own_ref[0], own_ref[1], next_refs[0][...], next_refs[1][...]]
    normed = [layer_norm_t(f.astype(jnp.float32)) for f in frames]
    own_n = jnp.concatenate([normed[2], normed[3]], axis=1)
    qkv = jnp.dot(wqkv_ref[...], own_n, preferred_element_type=jnp.float32).astype(jnp.bfloat16)
    nb_n = jnp.concatenate([normed[0], normed[1], normed[4], normed[5]], axis=1)
    kv_nb = jnp.dot(
        wqkv_ref[chans:, :], nb_n, preferred_element_type=jnp.float32
    ).astype(jnp.bfloat16)
    keys = [None] * 6
    vals = [None] * 6
    for w, slot in ((0, 0), (1, 1), (4, 2), (5, 3)):
        keys[w] = kv_nb[:chans, slot * block : (slot + 1) * block]
        vals[w] = kv_nb[chans:, slot * block : (slot + 1) * block]
    for t in range(2):
        keys[2 + t] = qkv[chans : 2 * chans, t * block : (t + 1) * block]
        vals[2 + t] = qkv[2 * chans :, t * block : (t + 1) * block]
    outs = []
    for t in range(2):
        q = qkv[:chans, t * block : (t + 1) * block].astype(jnp.float32)
        scores = []
        for d in range(5):
            w = t + d
            prod = q * keys[w].astype(jnp.float32)
            score = jnp.sum(prod.reshape(heads, HEAD_DIM, block), axis=1)
            score = score * (HEAD_DIM ** (-0.5))
            score = jnp.where(valid_ref[w] > 0, score, jnp.float32(-1e30))
            scores.append(score)
        top = scores[0]
        for s in scores[1:]:
            top = jnp.maximum(top, s)
        expo = [jnp.exp(s - top) for s in scores]
        denom = expo[0]
        for e in expo[1:]:
            denom = denom + e
        mixed = None
        for d in range(5):
            weight = (expo[d] / denom).astype(jnp.bfloat16).astype(jnp.float32)
            wide = jnp.broadcast_to(weight[:, None, :], (heads, HEAD_DIM, block)).reshape(chans, block)
            term = wide * vals[t + d].astype(jnp.float32)
            mixed = term if mixed is None else mixed + term
        outs.append(mixed.astype(jnp.bfloat16))
    attended = jnp.concatenate(outs, axis=1)
    proj = jnp.dot(wout_ref[...], attended, preferred_element_type=jnp.float32)
    xown = jnp.concatenate([own_ref[0], own_ref[1]], axis=1).astype(jnp.float32)
    hidden = (xown + proj).astype(jnp.bfloat16)
    out_ref[0] = hidden[:, :block]
    out_ref[1] = hidden[:, block:]


def attend(valid, prev, own, nxt0, nxt1, w_qkv, w_out):
    frames, chans, points = own.shape
    grid = (points // BLOCK,)
    assert points % BLOCK == 0
    cell_spec = pl.BlockSpec((frames, chans, BLOCK), lambda i: (0, 0, i))
    frame_spec = pl.BlockSpec((1, chans, BLOCK), lambda i: (0, 0, i))
    full = lambda shape: pl.BlockSpec(shape, lambda i: (0, 0))
    w_qkv = w_qkv.T
    w_out = w_out.T
    return pl.pallas_call(
        attend_kernel,
        grid=grid,
        in_specs=[
            pl.BlockSpec(memory_space=pltpu.SMEM),
            cell_spec,
            cell_spec,
            frame_spec,
            frame_spec,
            full(w_qkv.shape),
            full(w_out.shape),
        ],
        out_specs=cell_spec,
        out_shape=jax.ShapeDtypeStruct(own.shape, jnp.bfloat16),
    )(valid, prev, own, nxt0, nxt1, w_qkv, w_out)


def shift(x, axis, step):
    count = lax.axis_size(axis)
    if step > 0:
        pairs = [(i, i + 1) for i in range(count - 1)]
    else:
        pairs = [(i + 1, i) for i in range(count - 1)]
    return lax.ppermute(x, axis, pairs)


def swap(send_even, send_odd, axis, offset):
    count = lax.axis_size(axis)
    pairs = []
    for i in range(offset, count - 1, 2):
        pairs += [(i, i + 1), (i + 1, i)]
    even = lax.axis_index(axis) % 2 == 0
    if offset:
        payload = jnp.where(even, send_odd, send_even)
    else:
        payload = jnp.where(even, send_even, send_odd)
    return lax.ppermute(payload, axis, pairs)


def exchange(to_next, to_prev, axis):
    even = lax.axis_index(axis) % 2 == 0
    got_a = swap(to_next, to_prev, axis, 0)
    if lax.axis_size(axis) <= 2:
        zero = jnp.zeros_like(got_a)
        return jnp.where(even, zero, got_a), jnp.where(even, got_a, zero)
    got_b = swap(to_next, to_prev, axis, 1)
    from_prev = jnp.where(even, got_b, got_a)
    from_next = jnp.where(even, got_a, got_b)
    return from_prev, from_next


def body(latents, w_qkv, w_out, conv_weight):
    frames, rows, merged = latents.shape
    chans = w_out.shape[0]
    cols = merged // chans
    points = rows * cols
    cells = lambda a: a.reshape(frames, rows, cols, chans).transpose(0, 3, 1, 2).reshape(
        frames, chans, points
    )
    own_c = cells(latents)
    got_a = swap(own_c, own_c, "tm", 0)
    got_b0 = swap(own_c[:1], own_c[:1], "tm", 1)
    got_b1 = swap(own_c[1:], own_c[1:], "tm", 1)
    first = lax.axis_index("tm") * frames
    total = lax.axis_size("tm") * frames
    where_t = first + jnp.arange(6, dtype=jnp.int32) - 2
    valid = ((where_t >= 0) & (where_t < total)).astype(jnp.int32)
    even = (lax.axis_index("tm") % 2 == 0).astype(jnp.int32)
    valid = jnp.concatenate([valid, even[None]])
    hidden = attend(valid, got_a, own_c, got_b0, got_b1, w_qkv, w_out)
    hid = (
        hidden.reshape(frames, chans, rows, cols).transpose(0, 2, 3, 1).reshape(frames, rows, merged)
    )

    halo_top, halo_bot = exchange(hid[:, rows - 1 :, :], hid[:, :1, :], "row")
    tall = jnp.concatenate([halo_top, hid, halo_bot], axis=1)
    halo_left, halo_right = exchange(tall[:, :, merged - chans :], tall[:, :, :chans], "col")
    padded = jnp.concatenate([halo_left, tall, halo_right], axis=2)
    taps = jnp.tile(conv_weight, (1, cols))
    acc = hid.astype(jnp.float32)
    for tap_a in range(3):
        for tap_b in range(3):
            acc = (
                acc
                + padded[:, tap_a : tap_a + rows, tap_b * chans : tap_b * chans + merged].astype(
                    jnp.float32
                )
                * taps[3 * tap_a + tap_b]
            )
    return acc.astype(jnp.bfloat16)


def solution(mesh):
    placed = (P("tm", "row", "col"), P(), P(), P())
    return jax.shard_map(
        body, mesh=mesh, in_specs=placed, out_specs=P("tm", "row", "col"), check_vma=False
    )
```

```python
import functools

import jax
import jax.numpy as jnp
from jax import lax
from jax.experimental import pallas as pl
from jax.experimental.pallas import tpu as pltpu
from jax.sharding import PartitionSpec as P

HEAD_DIM = 64
BLOCK = 512


def layer_norm_t(cols):
    mean = jnp.mean(cols, axis=0, keepdims=True)
    cent = cols - mean
    var = jnp.mean(cent * cent, axis=0, keepdims=True)
    return (cent * lax.rsqrt(var + 1e-05)).astype(jnp.bfloat16)


def attend_kernel(valid_ref, a_ref, own_ref, b_ref, wqkv_ref, wout_ref, out_ref):
    @pl.when(valid_ref[6] > 0)
    def _():
        attend_body(valid_ref, b_ref, own_ref, a_ref, wqkv_ref, wout_ref, out_ref)

    @pl.when(valid_ref[6] == 0)
    def _():
        attend_body(valid_ref, a_ref, own_ref, b_ref, wqkv_ref, wout_ref, out_ref)


def attend_body(valid_ref, prev_ref, own_ref, next_ref, wqkv_ref, wout_ref, out_ref):
    chans = wout_ref.shape[0]
    heads = chans // HEAD_DIM
    block = own_ref.shape[2]
    frames = [prev_ref[0], prev_ref[1], own_ref[0], own_ref[1], next_ref[0], next_ref[1]]
    normed = [layer_norm_t(f.astype(jnp.float32)) for f in frames]
    own_n = jnp.concatenate([normed[2], normed[3]], axis=1)
    qkv = jnp.dot(wqkv_ref[...], own_n, preferred_element_type=jnp.float32).astype(jnp.bfloat16)
    nb_n = jnp.concatenate([normed[0], normed[1], normed[4], normed[5]], axis=1)
    kv_nb = jnp.dot(
        wqkv_ref[chans:, :], nb_n, preferred_element_type=jnp.float32
    ).astype(jnp.bfloat16)
    keys = [None] * 6
    vals = [None] * 6
    for w, slot in ((0, 0), (1, 1), (4, 2), (5, 3)):
        keys[w] = kv_nb[:chans, slot * block : (slot + 1) * block]
        vals[w] = kv_nb[chans:, slot * block : (slot + 1) * block]
    for t in range(2):
        keys[2 + t] = qkv[chans : 2 * chans, t * block : (t + 1) * block]
        vals[2 + t] = qkv[2 * chans :, t * block : (t + 1) * block]
    outs = []
    for t in range(2):
        q = qkv[:chans, t * block : (t + 1) * block].astype(jnp.float32)
        scores = []
        for d in range(5):
            w = t + d
            prod = q * keys[w].astype(jnp.float32)
            score = jnp.sum(prod.reshape(heads, HEAD_DIM, block), axis=1)
            score = score * (HEAD_DIM ** (-0.5))
            score = jnp.where(valid_ref[w] > 0, score, jnp.float32(-1e30))
            scores.append(score)
        top = scores[0]
        for s in scores[1:]:
            top = jnp.maximum(top, s)
        expo = [jnp.exp(s - top) for s in scores]
        denom = expo[0]
        for e in expo[1:]:
            denom = denom + e
        mixed = None
        for d in range(5):
            weight = (expo[d] / denom).astype(jnp.bfloat16).astype(jnp.float32)
            wide = jnp.broadcast_to(weight[:, None, :], (heads, HEAD_DIM, block)).reshape(chans, block)
            term = wide * vals[t + d].astype(jnp.float32)
            mixed = term if mixed is None else mixed + term
        outs.append(mixed.astype(jnp.bfloat16))
    attended = jnp.concatenate(outs, axis=1)
    proj = jnp.dot(wout_ref[...], attended, preferred_element_type=jnp.float32)
    xown = jnp.concatenate([own_ref[0], own_ref[1]], axis=1).astype(jnp.float32)
    hidden = (xown + proj).astype(jnp.bfloat16)
    out_ref[0] = hidden[:, :block]
    out_ref[1] = hidden[:, block:]


def attend(valid, prev, own, nxt, w_qkv, w_out):
    frames, chans, points = own.shape
    grid = (1,)
    cell_spec = pl.BlockSpec((frames, chans, points), lambda i: (0, 0, i))
    full = lambda shape: pl.BlockSpec(shape, lambda i: (0, 0))
    w_qkv = w_qkv.T
    w_out = w_out.T
    return pl.pallas_call(
        attend_kernel,
        grid=grid,
        in_specs=[
            pl.BlockSpec(memory_space=pltpu.SMEM),
            cell_spec,
            cell_spec,
            cell_spec,
            full(w_qkv.shape),
            full(w_out.shape),
        ],
        out_specs=cell_spec,
        out_shape=jax.ShapeDtypeStruct(own.shape, jnp.bfloat16),
    )(valid, prev, own, nxt, w_qkv, w_out)


def shift(x, axis, step):
    count = lax.axis_size(axis)
    if step > 0:
        pairs = [(i, i + 1) for i in range(count - 1)]
    else:
        pairs = [(i + 1, i) for i in range(count - 1)]
    return lax.ppermute(x, axis, pairs)


def swap(send_even, send_odd, axis, offset):
    count = lax.axis_size(axis)
    pairs = []
    for i in range(offset, count - 1, 2):
        pairs += [(i, i + 1), (i + 1, i)]
    even = lax.axis_index(axis) % 2 == 0
    if offset:
        payload = jnp.where(even, send_odd, send_even)
    else:
        payload = jnp.where(even, send_even, send_odd)
    return lax.ppermute(payload, axis, pairs)


def exchange(to_next, to_prev, axis):
    even = lax.axis_index(axis) % 2 == 0
    got_a = swap(to_next, to_prev, axis, 0)
    if lax.axis_size(axis) <= 2:
        zero = jnp.zeros_like(got_a)
        return jnp.where(even, zero, got_a), jnp.where(even, got_a, zero)
    got_b = swap(to_next, to_prev, axis, 1)
    from_prev = jnp.where(even, got_b, got_a)
    from_next = jnp.where(even, got_a, got_b)
    return from_prev, from_next


def body(latents, w_qkv, w_out, conv_weight):
    frames, rows, merged = latents.shape
    chans = w_out.shape[0]
    cols = merged // chans
    points = rows * cols
    assert lax.axis_size("row") == 2
    upper = lax.axis_index("row") == 0
    edge_x = jnp.where(upper, latents[:, rows - 1 :], latents[:, :1])
    halo_x = lax.ppermute(edge_x, "row", [(0, 1), (1, 0)])
    ext = jnp.concatenate([latents, halo_x], axis=1)
    own_c = ext.reshape(frames, rows + 1, cols, chans).transpose(0, 3, 1, 2).reshape(
        frames, chans, points + cols
    )
    got_a = swap(own_c, own_c, "tm", 0)
    got_b = swap(own_c, own_c, "tm", 1)
    first = lax.axis_index("tm") * frames
    total = lax.axis_size("tm") * frames
    where_t = first + jnp.arange(6, dtype=jnp.int32) - 2
    valid = ((where_t >= 0) & (where_t < total)).astype(jnp.int32)
    even = (lax.axis_index("tm") % 2 == 0).astype(jnp.int32)
    valid = jnp.concatenate([valid, even[None]])
    hidden = attend(valid, got_a, own_c, got_b, w_qkv, w_out)
    hid = (
        hidden[:, :, :points]
        .reshape(frames, chans, rows, cols)
        .transpose(0, 2, 3, 1)
        .reshape(frames, rows, merged)
    )
    hrow = hidden[:, :, points:].transpose(0, 2, 1).reshape(frames, 1, merged)
    zero = jnp.zeros_like(hrow)
    halo_top = jnp.where(upper, zero, hrow)
    halo_bot = jnp.where(upper, hrow, zero)
    tall = jnp.concatenate([halo_top, hid, halo_bot], axis=1)
    halo_left, halo_right = exchange(tall[:, :, merged - chans :], tall[:, :, :chans], "col")
    padded = jnp.concatenate([halo_left, tall, halo_right], axis=2)
    taps = jnp.tile(conv_weight, (1, cols))
    acc = hid.astype(jnp.float32)
    for tap_a in range(3):
        for tap_b in range(3):
            acc = (
                acc
                + padded[:, tap_a : tap_a + rows, tap_b * chans : tap_b * chans + merged].astype(
                    jnp.float32
                )
                * taps[3 * tap_a + tap_b]
            )
    return acc.astype(jnp.bfloat16)


def solution(mesh):
    placed = (P("tm", "row", "col"), P(), P(), P())
    return jax.shard_map(
        body, mesh=mesh, in_specs=placed, out_specs=P("tm", "row", "col"), check_vma=False
    )
```

```python
import functools

import jax
import jax.numpy as jnp
from jax import lax
from jax.experimental import pallas as pl
from jax.experimental.pallas import tpu as pltpu
from jax.sharding import PartitionSpec as P

HEAD_DIM = 64
BLOCK = 512


def layer_norm_t(cols):
    mean = jnp.mean(cols, axis=0, keepdims=True)
    cent = cols - mean
    var = jnp.mean(cent * cent, axis=0, keepdims=True)
    return (cent * lax.rsqrt(var + 1e-05)).astype(jnp.bfloat16)


def attend_kernel(valid_ref, a_ref, own_ref, b_ref, wqkv_ref, wout_ref, out_ref):
    @pl.when(valid_ref[6] > 0)
    def _():
        attend_body(valid_ref, b_ref, own_ref, a_ref, wqkv_ref, wout_ref, out_ref)

    @pl.when(valid_ref[6] == 0)
    def _():
        attend_body(valid_ref, a_ref, own_ref, b_ref, wqkv_ref, wout_ref, out_ref)


def attend_body(valid_ref, prev_ref, own_ref, next_ref, wqkv_ref, wout_ref, out_ref):
    chans = wout_ref.shape[0]
    heads = chans // HEAD_DIM
    block = own_ref.shape[2]
    frames = [prev_ref[0], prev_ref[1], own_ref[0], own_ref[1], next_ref[0], next_ref[1]]
    normed = [layer_norm_t(f.astype(jnp.float32)) for f in frames]
    own_n = jnp.concatenate([normed[2], normed[3]], axis=1)
    qkv = jnp.dot(wqkv_ref[...], own_n, preferred_element_type=jnp.float32).astype(jnp.bfloat16)
    nb_n = jnp.concatenate([normed[0], normed[1], normed[4], normed[5]], axis=1)
    kv_nb = jnp.dot(
        wqkv_ref[chans:, :], nb_n, preferred_element_type=jnp.float32
    ).astype(jnp.bfloat16)
    keys = [None] * 6
    vals = [None] * 6
    for w, slot in ((0, 0), (1, 1), (4, 2), (5, 3)):
        keys[w] = kv_nb[:chans, slot * block : (slot + 1) * block]
        vals[w] = kv_nb[chans:, slot * block : (slot + 1) * block]
    for t in range(2):
        keys[2 + t] = qkv[chans : 2 * chans, t * block : (t + 1) * block]
        vals[2 + t] = qkv[2 * chans :, t * block : (t + 1) * block]
    outs = []
    for t in range(2):
        q = qkv[:chans, t * block : (t + 1) * block].astype(jnp.float32)
        scores = []
        for d in range(5):
            w = t + d
            prod = q * keys[w].astype(jnp.float32)
            score = jnp.sum(prod.reshape(heads, HEAD_DIM, block), axis=1)
            score = score * (HEAD_DIM ** (-0.5))
            score = jnp.where(valid_ref[w] > 0, score, jnp.float32(-1e30))
            scores.append(score)
        top = scores[0]
        for s in scores[1:]:
            top = jnp.maximum(top, s)
        expo = [jnp.exp(s - top) for s in scores]
        denom = expo[0]
        for e in expo[1:]:
            denom = denom + e
        mixed = None
        for d in range(5):
            weight = (expo[d] / denom).astype(jnp.bfloat16).astype(jnp.float32)
            wide = jnp.broadcast_to(weight[:, None, :], (heads, HEAD_DIM, block)).reshape(chans, block)
            term = wide * vals[t + d].astype(jnp.float32)
            mixed = term if mixed is None else mixed + term
        outs.append(mixed.astype(jnp.bfloat16))
    attended = jnp.concatenate(outs, axis=1)
    proj = jnp.dot(wout_ref[...], attended, preferred_element_type=jnp.float32)
    xown = jnp.concatenate([own_ref[0], own_ref[1]], axis=1).astype(jnp.float32)
    hidden = (xown + proj).astype(jnp.bfloat16)
    out_ref[0] = hidden[:, :block]
    out_ref[1] = hidden[:, block:]


def attend(valid, prev, own, nxt, w_qkv, w_out):
    frames, chans, points = own.shape
    grid = (points // BLOCK,)
    assert points % BLOCK == 0
    cell_spec = pl.BlockSpec((frames, chans, BLOCK), lambda i: (0, 0, i))
    full = lambda shape: pl.BlockSpec(shape, lambda i: (0, 0))
    w_qkv = w_qkv.T
    w_out = w_out.T
    return pl.pallas_call(
        attend_kernel,
        grid=grid,
        in_specs=[
            pl.BlockSpec(memory_space=pltpu.SMEM),
            cell_spec,
            cell_spec,
            cell_spec,
            full(w_qkv.shape),
            full(w_out.shape),
        ],
        out_specs=cell_spec,
        out_shape=jax.ShapeDtypeStruct(own.shape, jnp.bfloat16),
    )(valid, prev, own, nxt, w_qkv, w_out)


def shift(x, axis, step):
    count = lax.axis_size(axis)
    if step > 0:
        pairs = [(i, i + 1) for i in range(count - 1)]
    else:
        pairs = [(i + 1, i) for i in range(count - 1)]
    return lax.ppermute(x, axis, pairs)


def swap(send_even, send_odd, axis, offset):
    count = lax.axis_size(axis)
    pairs = []
    for i in range(offset, count - 1, 2):
        pairs += [(i, i + 1), (i + 1, i)]
    even = lax.axis_index(axis) % 2 == 0
    if offset:
        payload = jnp.where(even, send_odd, send_even)
    else:
        payload = jnp.where(even, send_even, send_odd)
    return lax.ppermute(payload, axis, pairs)


def exchange(to_next, to_prev, axis):
    even = lax.axis_index(axis) % 2 == 0
    got_a = swap(to_next, to_prev, axis, 0)
    if lax.axis_size(axis) <= 2:
        zero = jnp.zeros_like(got_a)
        return jnp.where(even, zero, got_a), jnp.where(even, got_a, zero)
    got_b = swap(to_next, to_prev, axis, 1)
    from_prev = jnp.where(even, got_b, got_a)
    from_next = jnp.where(even, got_a, got_b)
    return from_prev, from_next


def body(latents, w_qkv, w_out, conv_weight):
    frames, rows, merged = latents.shape
    chans = w_out.shape[0]
    cols = merged // chans
    points = rows * cols
    cells = lambda a: a.reshape(frames, rows, cols, chans).transpose(0, 3, 1, 2).reshape(
        frames, chans, points
    )
    raw_b = swap(latents, latents, "tm", 1)
    own_c = cells(latents)
    got_a = swap(own_c, own_c, "tm", 0)
    got_b = cells(raw_b)
    first = lax.axis_index("tm") * frames
    total = lax.axis_size("tm") * frames
    where_t = first + jnp.arange(6, dtype=jnp.int32) - 2
    valid = ((where_t >= 0) & (where_t < total)).astype(jnp.int32)
    even = (lax.axis_index("tm") % 2 == 0).astype(jnp.int32)
    valid = jnp.concatenate([valid, even[None]])
    hidden = attend(valid, got_a, own_c, got_b, w_qkv, w_out)
    hid = (
        hidden.reshape(frames, chans, rows, cols).transpose(0, 2, 3, 1).reshape(frames, rows, merged)
    )

    halo_top, halo_bot = exchange(hid[:, rows - 1 :, :], hid[:, :1, :], "row")
    tall = jnp.concatenate([halo_top, hid, halo_bot], axis=1)
    halo_left, halo_right = exchange(tall[:, :, merged - chans :], tall[:, :, :chans], "col")
    padded = jnp.concatenate([halo_left, tall, halo_right], axis=2)
    taps = jnp.tile(conv_weight, (1, cols))
    acc = hid.astype(jnp.float32)
    for tap_a in range(3):
        for tap_b in range(3):
            acc = (
                acc
                + padded[:, tap_a : tap_a + rows, tap_b * chans : tap_b * chans + merged].astype(
                    jnp.float32
                )
                * taps[3 * tap_a + tap_b]
            )
    return acc.astype(jnp.bfloat16)


def solution(mesh):
    placed = (P("tm", "row", "col"), P(), P(), P())
    return jax.shard_map(
        body, mesh=mesh, in_specs=placed, out_specs=P("tm", "row", "col"), check_vma=False
    )
```

```python
import functools

import jax
import jax.numpy as jnp
from jax import lax
from jax.experimental import pallas as pl
from jax.experimental.pallas import tpu as pltpu
from jax.sharding import PartitionSpec as P

HEAD_DIM = 64
BLOCK = 512


def layer_norm_t(cols):
    mean = jnp.mean(cols, axis=0, keepdims=True)
    cent = cols - mean
    var = jnp.mean(cent * cent, axis=0, keepdims=True)
    return (cent * lax.rsqrt(var + 1e-05)).astype(jnp.bfloat16)


def attend_kernel(valid_ref, a_ref, own_ref, b_ref, wqkv_ref, wout_ref, out_ref):
    @pl.when(valid_ref[6] > 0)
    def _():
        attend_body(valid_ref, b_ref, own_ref, a_ref, wqkv_ref, wout_ref, out_ref)

    @pl.when(valid_ref[6] == 0)
    def _():
        attend_body(valid_ref, a_ref, own_ref, b_ref, wqkv_ref, wout_ref, out_ref)


def attend_body(valid_ref, prev_ref, own_ref, next_ref, wqkv_ref, wout_ref, out_ref):
    chans = wout_ref.shape[0]
    heads = chans // HEAD_DIM
    block = own_ref.shape[2]
    frames = [prev_ref[0], prev_ref[1], own_ref[0], own_ref[1], next_ref[0], next_ref[1]]
    normed = [layer_norm_t(f.astype(jnp.float32)) for f in frames]
    own_n = jnp.concatenate([normed[2], normed[3]], axis=1)
    qkv = jnp.dot(wqkv_ref[...], own_n, preferred_element_type=jnp.float32).astype(jnp.bfloat16)
    nb_n = jnp.concatenate([normed[0], normed[1], normed[4], normed[5]], axis=1)
    kv_nb = jnp.dot(
        wqkv_ref[chans:, :], nb_n, preferred_element_type=jnp.float32
    ).astype(jnp.bfloat16)
    keys = [None] * 6
    vals = [None] * 6
    for w, slot in ((0, 0), (1, 1), (4, 2), (5, 3)):
        keys[w] = kv_nb[:chans, slot * block : (slot + 1) * block]
        vals[w] = kv_nb[chans:, slot * block : (slot + 1) * block]
    for t in range(2):
        keys[2 + t] = qkv[chans : 2 * chans, t * block : (t + 1) * block]
        vals[2 + t] = qkv[2 * chans :, t * block : (t + 1) * block]
    outs = []
    for t in range(2):
        q = qkv[:chans, t * block : (t + 1) * block].astype(jnp.float32)
        scores = []
        for d in range(5):
            w = t + d
            prod = q * keys[w].astype(jnp.float32)
            score = jnp.sum(prod.reshape(heads, HEAD_DIM, block), axis=1)
            score = score * (HEAD_DIM ** (-0.5))
            score = jnp.where(valid_ref[w] > 0, score, jnp.float32(-1e30))
            scores.append(score)
        top = scores[0]
        for s in scores[1:]:
            top = jnp.maximum(top, s)
        expo = [jnp.exp(s - top) for s in scores]
        denom = expo[0]
        for e in expo[1:]:
            denom = denom + e
        mixed = None
        for d in range(5):
            weight = (expo[d] / denom).astype(jnp.bfloat16).astype(jnp.float32)
            wide = jnp.broadcast_to(weight[:, None, :], (heads, HEAD_DIM, block)).reshape(chans, block)
            term = wide * vals[t + d].astype(jnp.float32)
            mixed = term if mixed is None else mixed + term
        outs.append(mixed.astype(jnp.bfloat16))
    attended = jnp.concatenate(outs, axis=1)
    proj = jnp.dot(wout_ref[...], attended, preferred_element_type=jnp.float32)
    xown = jnp.concatenate([own_ref[0], own_ref[1]], axis=1).astype(jnp.float32)
    hidden = (xown + proj).astype(jnp.bfloat16)
    out_ref[0] = hidden[:, :block]
    out_ref[1] = hidden[:, block:]


def attend(valid, prev, own, nxt, w_qkv, w_out):
    frames, chans, points = own.shape
    grid = (points // BLOCK,)
    assert points % BLOCK == 0
    cell_spec = pl.BlockSpec((frames, chans, BLOCK), lambda i: (0, 0, i))
    full = lambda shape: pl.BlockSpec(shape, lambda i: (0, 0))
    w_qkv = w_qkv.T
    w_out = w_out.T
    return pl.pallas_call(
        attend_kernel,
        grid=grid,
        in_specs=[
            pl.BlockSpec(memory_space=pltpu.SMEM),
            cell_spec,
            cell_spec,
            cell_spec,
            full(w_qkv.shape),
            full(w_out.shape),
        ],
        out_specs=cell_spec,
        out_shape=jax.ShapeDtypeStruct(own.shape, jnp.bfloat16),
    )(valid, prev, own, nxt, w_qkv, w_out)


def shift(x, axis, step):
    count = lax.axis_size(axis)
    if step > 0:
        pairs = [(i, i + 1) for i in range(count - 1)]
    else:
        pairs = [(i + 1, i) for i in range(count - 1)]
    return lax.ppermute(x, axis, pairs)


def swap(send_even, send_odd, axis, offset):
    count = lax.axis_size(axis)
    pairs = []
    for i in range(offset, count - 1, 2):
        pairs += [(i, i + 1), (i + 1, i)]
    even = lax.axis_index(axis) % 2 == 0
    if offset:
        payload = jnp.where(even, send_odd, send_even)
    else:
        payload = jnp.where(even, send_even, send_odd)
    return lax.ppermute(payload, axis, pairs)


def exchange(to_next, to_prev, axis):
    even = lax.axis_index(axis) % 2 == 0
    got_a = swap(to_next, to_prev, axis, 0)
    if lax.axis_size(axis) <= 2:
        zero = jnp.zeros_like(got_a)
        return jnp.where(even, zero, got_a), jnp.where(even, got_a, zero)
    got_b = swap(to_next, to_prev, axis, 1)
    from_prev = jnp.where(even, got_b, got_a)
    from_next = jnp.where(even, got_a, got_b)
    return from_prev, from_next


def body(latents, w_qkv, w_out, conv_weight):
    frames, rows, merged = latents.shape
    chans = w_out.shape[0]
    cols = merged // chans
    points = rows * cols
    cells = lambda a: a.reshape(frames, rows, cols, chans).transpose(0, 3, 1, 2).reshape(
        frames, chans, points
    )
    raw_b = swap(latents, latents, "tm", 1)
    own_c = cells(latents)
    got_a = swap(own_c, own_c, "tm", 0)
    got_b = cells(raw_b)
    first = lax.axis_index("tm") * frames
    total = lax.axis_size("tm") * frames
    where_t = first + jnp.arange(6, dtype=jnp.int32) - 2
    valid = ((where_t >= 0) & (where_t < total)).astype(jnp.int32)
    even = (lax.axis_index("tm") % 2 == 0).astype(jnp.int32)
    valid = jnp.concatenate([valid, even[None]])
    hidden = attend(valid, got_a, own_c, got_b, w_qkv, w_out)
    hid = (
        hidden.reshape(frames, chans, rows, cols).transpose(0, 2, 3, 1).reshape(frames, rows, merged)
    )

    as_row = lambda a: a.transpose(0, 2, 1).reshape(frames, 1, merged)
    edge_top, edge_bot = exchange(hidden[:, :, points - cols :], hidden[:, :, :cols], "row")
    halo_top, halo_bot = as_row(edge_top), as_row(edge_bot)
    tall = jnp.concatenate([halo_top, hid, halo_bot], axis=1)
    halo_left, halo_right = exchange(tall[:, :, merged - chans :], tall[:, :, :chans], "col")
    padded = jnp.concatenate([halo_left, tall, halo_right], axis=2)
    taps = jnp.tile(conv_weight, (1, cols))
    acc = hid.astype(jnp.float32)
    for tap_a in range(3):
        for tap_b in range(3):
            acc = (
                acc
                + padded[:, tap_a : tap_a + rows, tap_b * chans : tap_b * chans + merged].astype(
                    jnp.float32
                )
                * taps[3 * tap_a + tap_b]
            )
    return acc.astype(jnp.bfloat16)


def solution(mesh):
    placed = (P("tm", "row", "col"), P(), P(), P())
    return jax.shard_map(
        body, mesh=mesh, in_specs=placed, out_specs=P("tm", "row", "col"), check_vma=False
    )
```

```python
import functools

import jax
import jax.numpy as jnp
from jax import lax
from jax.experimental import pallas as pl
from jax.experimental.pallas import tpu as pltpu
from jax.sharding import PartitionSpec as P

HEAD_DIM = 64
BLOCK = 512


def layer_norm_t(cols):
    mean = jnp.mean(cols, axis=0, keepdims=True)
    cent = cols - mean
    var = jnp.mean(cent * cent, axis=0, keepdims=True)
    return (cent * lax.rsqrt(var + 1e-05)).astype(jnp.bfloat16)


def attend_kernel(valid_ref, a_ref, own_ref, b_ref, wqkv_ref, wout_ref, out_ref):
    @pl.when(valid_ref[6] > 0)
    def _():
        attend_body(valid_ref, b_ref, own_ref, a_ref, wqkv_ref, wout_ref, out_ref)

    @pl.when(valid_ref[6] == 0)
    def _():
        attend_body(valid_ref, a_ref, own_ref, b_ref, wqkv_ref, wout_ref, out_ref)


def attend_body(valid_ref, prev_ref, own_ref, next_ref, wqkv_ref, wout_ref, out_ref):
    chans = wout_ref.shape[0]
    heads = chans // HEAD_DIM
    block = own_ref.shape[2]
    frames = [prev_ref[0], prev_ref[1], own_ref[0], own_ref[1], next_ref[0], next_ref[1]]
    normed = [layer_norm_t(f.astype(jnp.float32)) for f in frames]
    own_n = jnp.concatenate([normed[2], normed[3]], axis=1)
    qkv = jnp.dot(wqkv_ref[...], own_n, preferred_element_type=jnp.float32).astype(jnp.bfloat16)
    nb_n = jnp.concatenate([normed[0], normed[1], normed[4], normed[5]], axis=1)
    kv_nb = jnp.dot(
        wqkv_ref[chans:, :], nb_n, preferred_element_type=jnp.float32
    ).astype(jnp.bfloat16)
    keys = [None] * 6
    vals = [None] * 6
    for w, slot in ((0, 0), (1, 1), (4, 2), (5, 3)):
        keys[w] = kv_nb[:chans, slot * block : (slot + 1) * block]
        vals[w] = kv_nb[chans:, slot * block : (slot + 1) * block]
    for t in range(2):
        keys[2 + t] = qkv[chans : 2 * chans, t * block : (t + 1) * block]
        vals[2 + t] = qkv[2 * chans :, t * block : (t + 1) * block]
    outs = []
    for t in range(2):
        q = qkv[:chans, t * block : (t + 1) * block].astype(jnp.float32)
        scores = []
        for d in range(5):
            w = t + d
            prod = q * keys[w].astype(jnp.float32)
            score = jnp.sum(prod.reshape(heads, HEAD_DIM, block), axis=1)
            score = score * (HEAD_DIM ** (-0.5))
            score = jnp.where(valid_ref[w] > 0, score, jnp.float32(-1e30))
            scores.append(score)
        top = scores[0]
        for s in scores[1:]:
            top = jnp.maximum(top, s)
        expo = [jnp.exp(s - top) for s in scores]
        denom = expo[0]
        for e in expo[1:]:
            denom = denom + e
        mixed = None
        for d in range(5):
            weight = (expo[d] / denom).astype(jnp.bfloat16).astype(jnp.float32)
            wide = jnp.broadcast_to(weight[:, None, :], (heads, HEAD_DIM, block)).reshape(chans, block)
            term = wide * vals[t + d].astype(jnp.float32)
            mixed = term if mixed is None else mixed + term
        outs.append(mixed.astype(jnp.bfloat16))
    attended = jnp.concatenate(outs, axis=1)
    proj = jnp.dot(wout_ref[...], attended, preferred_element_type=jnp.float32)
    xown = jnp.concatenate([own_ref[0], own_ref[1]], axis=1).astype(jnp.float32)
    hidden = (xown + proj).astype(jnp.bfloat16)
    out_ref[0] = hidden[:, :block]
    out_ref[1] = hidden[:, block:]


def attend(valid, prev, own, nxt, w_qkv, w_out):
    frames, chans, points = own.shape
    grid = (points // BLOCK,)
    assert points % BLOCK == 0
    cell_spec = pl.BlockSpec((frames, chans, BLOCK), lambda i: (0, 0, i))
    full = lambda shape: pl.BlockSpec(shape, lambda i: (0, 0))
    w_qkv = w_qkv.T
    w_out = w_out.T
    return pl.pallas_call(
        attend_kernel,
        grid=grid,
        in_specs=[
            pl.BlockSpec(memory_space=pltpu.SMEM),
            cell_spec,
            cell_spec,
            cell_spec,
            full(w_qkv.shape),
            full(w_out.shape),
        ],
        out_specs=cell_spec,
        out_shape=jax.ShapeDtypeStruct(own.shape, jnp.bfloat16),
    )(valid, prev, own, nxt, w_qkv, w_out)


def shift(x, axis, step):
    count = lax.axis_size(axis)
    if step > 0:
        pairs = [(i, i + 1) for i in range(count - 1)]
    else:
        pairs = [(i + 1, i) for i in range(count - 1)]
    return lax.ppermute(x, axis, pairs)


def swap(send_even, send_odd, axis, offset):
    count = lax.axis_size(axis)
    pairs = []
    for i in range(offset, count - 1, 2):
        pairs += [(i, i + 1), (i + 1, i)]
    even = lax.axis_index(axis) % 2 == 0
    if offset:
        payload = jnp.where(even, send_odd, send_even)
    else:
        payload = jnp.where(even, send_even, send_odd)
    return lax.ppermute(payload, axis, pairs)


def exchange(to_next, to_prev, axis):
    even = lax.axis_index(axis) % 2 == 0
    got_a = swap(to_next, to_prev, axis, 0)
    if lax.axis_size(axis) <= 2:
        zero = jnp.zeros_like(got_a)
        return jnp.where(even, zero, got_a), jnp.where(even, got_a, zero)
    got_b = swap(to_next, to_prev, axis, 1)
    from_prev = jnp.where(even, got_b, got_a)
    from_next = jnp.where(even, got_a, got_b)
    return from_prev, from_next


def body(latents, w_qkv, w_out, conv_weight):
    frames, rows, merged = latents.shape
    chans = w_out.shape[0]
    cols = merged // chans
    points = rows * cols
    cells = lambda a: a.reshape(frames, rows, cols, chans).transpose(0, 3, 1, 2).reshape(
        frames, chans, points
    )
    raw_b = swap(latents, latents, "tm", 1)
    own_c = cells(latents)
    got_a = swap(own_c, own_c, "tm", 0)
    got_b = cells(raw_b)
    first = lax.axis_index("tm") * frames
    total = lax.axis_size("tm") * frames
    where_t = first + jnp.arange(6, dtype=jnp.int32) - 2
    valid = ((where_t >= 0) & (where_t < total)).astype(jnp.int32)
    even = (lax.axis_index("tm") % 2 == 0).astype(jnp.int32)
    valid = jnp.concatenate([valid, even[None]])
    hidden = attend(valid, got_a, own_c, got_b, w_qkv, w_out)
    hid = (
        hidden.reshape(frames, chans, rows, cols).transpose(0, 2, 3, 1).reshape(frames, rows, merged)
    )

    halo_left, halo_right = exchange(hid[:, :, merged - chans :], hid[:, :, :chans], "col")
    wide = jnp.concatenate([halo_left, hid, halo_right], axis=2)
    halo_top, halo_bot = exchange(wide[:, rows - 1 :, :], wide[:, :1, :], "row")
    padded = jnp.concatenate([halo_top, wide, halo_bot], axis=1)
    taps = jnp.tile(conv_weight, (1, cols))
    acc = hid.astype(jnp.float32)
    for tap_a in range(3):
        for tap_b in range(3):
            acc = (
                acc
                + padded[:, tap_a : tap_a + rows, tap_b * chans : tap_b * chans + merged].astype(
                    jnp.float32
                )
                * taps[3 * tap_a + tap_b]
            )
    return acc.astype(jnp.bfloat16)


def solution(mesh):
    placed = (P("tm", "row", "col"), P(), P(), P())
    return jax.shard_map(
        body, mesh=mesh, in_specs=placed, out_specs=P("tm", "row", "col"), check_vma=False
    )
```

```python
import functools

import jax
import jax.numpy as jnp
from jax import lax
from jax.experimental import pallas as pl
from jax.experimental.pallas import tpu as pltpu
from jax.sharding import PartitionSpec as P

HEAD_DIM = 64
BLOCK = 512


def layer_norm_t(cols):
    mean = jnp.mean(cols, axis=0, keepdims=True)
    cent = cols - mean
    var = jnp.mean(cent * cent, axis=0, keepdims=True)
    return (cent * lax.rsqrt(var + 1e-05)).astype(jnp.bfloat16)


def attend_kernel(valid_ref, a_ref, own_ref, b_ref, wqkv_ref, wout_ref, out_ref):
    @pl.when(valid_ref[6] > 0)
    def _():
        attend_body(valid_ref, b_ref, own_ref, a_ref, wqkv_ref, wout_ref, out_ref)

    @pl.when(valid_ref[6] == 0)
    def _():
        attend_body(valid_ref, a_ref, own_ref, b_ref, wqkv_ref, wout_ref, out_ref)


def attend_body(valid_ref, prev_ref, own_ref, next_ref, wqkv_ref, wout_ref, out_ref):
    chans = wout_ref.shape[0]
    heads = chans // HEAD_DIM
    block = own_ref.shape[2]
    frames = [prev_ref[0], prev_ref[1], own_ref[0], own_ref[1], next_ref[0], next_ref[1]]
    normed = [layer_norm_t(f.astype(jnp.float32)) for f in frames]
    own_n = jnp.concatenate([normed[2], normed[3]], axis=1)
    qkv = jnp.dot(wqkv_ref[...], own_n, preferred_element_type=jnp.float32).astype(jnp.bfloat16)
    nb_n = jnp.concatenate([normed[0], normed[1], normed[4], normed[5]], axis=1)
    kv_nb = jnp.dot(
        wqkv_ref[chans:, :], nb_n, preferred_element_type=jnp.float32
    ).astype(jnp.bfloat16)
    keys = [None] * 6
    vals = [None] * 6
    for w, slot in ((0, 0), (1, 1), (4, 2), (5, 3)):
        keys[w] = kv_nb[:chans, slot * block : (slot + 1) * block]
        vals[w] = kv_nb[chans:, slot * block : (slot + 1) * block]
    for t in range(2):
        keys[2 + t] = qkv[chans : 2 * chans, t * block : (t + 1) * block]
        vals[2 + t] = qkv[2 * chans :, t * block : (t + 1) * block]
    outs = []
    for t in range(2):
        q = qkv[:chans, t * block : (t + 1) * block].astype(jnp.float32)
        scores = []
        for d in range(5):
            w = t + d
            prod = q * keys[w].astype(jnp.float32)
            score = jnp.concatenate(
                [
                    jnp.sum(prod[h * HEAD_DIM : (h + 1) * HEAD_DIM], axis=0, keepdims=True)
                    for h in range(heads)
                ],
                axis=0,
            )
            score = score * (HEAD_DIM ** (-0.5))
            score = jnp.where(valid_ref[w] > 0, score, jnp.float32(-1e30))
            scores.append(score)
        top = scores[0]
        for s in scores[1:]:
            top = jnp.maximum(top, s)
        expo = [jnp.exp(s - top) for s in scores]
        denom = expo[0]
        for e in expo[1:]:
            denom = denom + e
        mixed = None
        for d in range(5):
            weight = (expo[d] / denom).astype(jnp.bfloat16).astype(jnp.float32)
            vt = vals[t + d].astype(jnp.float32)
            term = jnp.concatenate(
                [weight[h : h + 1] * vt[h * HEAD_DIM : (h + 1) * HEAD_DIM] for h in range(heads)],
                axis=0,
            )
            mixed = term if mixed is None else mixed + term
        outs.append(mixed.astype(jnp.bfloat16))
    attended = jnp.concatenate(outs, axis=1)
    proj = jnp.dot(wout_ref[...], attended, preferred_element_type=jnp.float32)
    xown = jnp.concatenate([own_ref[0], own_ref[1]], axis=1).astype(jnp.float32)
    hidden = (xown + proj).astype(jnp.bfloat16)
    out_ref[0] = hidden[:, :block]
    out_ref[1] = hidden[:, block:]


def attend(valid, prev, own, nxt, w_qkv, w_out):
    frames, chans, points = own.shape
    grid = (points // BLOCK,)
    assert points % BLOCK == 0
    cell_spec = pl.BlockSpec((frames, chans, BLOCK), lambda i: (0, 0, i))
    full = lambda shape: pl.BlockSpec(shape, lambda i: (0, 0))
    w_qkv = w_qkv.T
    w_out = w_out.T
    return pl.pallas_call(
        attend_kernel,
        grid=grid,
        in_specs=[
            pl.BlockSpec(memory_space=pltpu.SMEM),
            cell_spec,
            cell_spec,
            cell_spec,
            full(w_qkv.shape),
            full(w_out.shape),
        ],
        out_specs=cell_spec,
        out_shape=jax.ShapeDtypeStruct(own.shape, jnp.bfloat16),
        compiler_params=pltpu.CompilerParams(),
    )(valid, prev, own, nxt, w_qkv, w_out)


def shift(x, axis, step):
    count = lax.axis_size(axis)
    if step > 0:
        pairs = [(i, i + 1) for i in range(count - 1)]
    else:
        pairs = [(i + 1, i) for i in range(count - 1)]
    return lax.ppermute(x, axis, pairs)


def swap(send_even, send_odd, axis, offset):
    count = lax.axis_size(axis)
    pairs = []
    for i in range(offset, count - 1, 2):
        pairs += [(i, i + 1), (i + 1, i)]
    even = lax.axis_index(axis) % 2 == 0
    if offset:
        payload = jnp.where(even, send_odd, send_even)
    else:
        payload = jnp.where(even, send_even, send_odd)
    return lax.ppermute(payload, axis, pairs)


def exchange(to_next, to_prev, axis):
    even = lax.axis_index(axis) % 2 == 0
    got_a = swap(to_next, to_prev, axis, 0)
    if lax.axis_size(axis) <= 2:
        zero = jnp.zeros_like(got_a)
        return jnp.where(even, zero, got_a), jnp.where(even, got_a, zero)
    got_b = swap(to_next, to_prev, axis, 1)
    from_prev = jnp.where(even, got_b, got_a)
    from_next = jnp.where(even, got_a, got_b)
    return from_prev, from_next


def body(latents, w_qkv, w_out, conv_weight):
    frames, rows, merged = latents.shape
    chans = w_out.shape[0]
    cols = merged // chans
    points = rows * cols
    cells = lambda a: a.reshape(frames, rows, cols, chans).transpose(0, 3, 1, 2).reshape(
        frames, chans, points
    )
    raw_b = swap(latents, latents, "tm", 1)
    own_c = cells(latents)
    got_a = swap(own_c, own_c, "tm", 0)
    got_b = cells(raw_b)
    first = lax.axis_index("tm") * frames
    total = lax.axis_size("tm") * frames
    where_t = first + jnp.arange(6, dtype=jnp.int32) - 2
    valid = ((where_t >= 0) & (where_t < total)).astype(jnp.int32)
    even = (lax.axis_index("tm") % 2 == 0).astype(jnp.int32)
    valid = jnp.concatenate([valid, even[None]])
    hidden = attend(valid, got_a, own_c, got_b, w_qkv, w_out)
    hid = (
        hidden.reshape(frames, chans, rows, cols).transpose(0, 2, 3, 1).reshape(frames, rows, merged)
    )

    halo_top, halo_bot = exchange(hid[:, rows - 1 :, :], hid[:, :1, :], "row")
    tall = jnp.concatenate([halo_top, hid, halo_bot], axis=1)
    halo_left, halo_right = exchange(tall[:, :, merged - chans :], tall[:, :, :chans], "col")
    padded = jnp.concatenate([halo_left, tall, halo_right], axis=2)
    taps = jnp.tile(conv_weight, (1, cols))
    acc = hid.astype(jnp.float32)
    for tap_a in range(3):
        for tap_b in range(3):
            acc = (
                acc
                + padded[:, tap_a : tap_a + rows, tap_b * chans : tap_b * chans + merged].astype(
                    jnp.float32
                )
                * taps[3 * tap_a + tap_b]
            )
    return acc.astype(jnp.bfloat16)


def solution(mesh):
    placed = (P("tm", "row", "col"), P(), P(), P())
    return jax.shard_map(
        body, mesh=mesh, in_specs=placed, out_specs=P("tm", "row", "col"), check_vma=False
    )
```
